128 devices in a mesh: ctx: 16 (over z, y), head: 8 (over x, core).
Axes of the slice: x: 4, y: 4, z: 4, core: 2. Of those that a mesh axis runs over, the one named last changes fastest.
Arguments:
- queries: bfloat16 [32768, 8192], P(('ctx', 'head')), may hold values from -150 to 150
- key_states: bfloat16 [32768, 1024], P(('ctx', 'head')), may hold values from -10 to 10
- value_states: bfloat16 [32768, 1024], P(('ctx', 'head')), may hold values from -6 to 6
- page_ids: int32 [256], replicated, may hold values from 0 to 63, never falling along the last dimension, each value on 1 to 8 neighbouring positions
- ref_group: int32 [256, 4], replicated, may hold values from 0 to 15, all different within a row; in each aligned block of 16 rows (0 to 15, 16 to 31, ...) at most 4 rows name the same one
- ref_slot: int32 [256, 4], replicated, may hold values from 0 to 15
Outputs:
- attended: bfloat16 [32768, 8192], P(('ctx', 'head'))
The draws below stay inside these ranges and needn't reach their ends.
Inputs may be any that keep to these rules, and one draw needn't show every extreme that they name: `page_ids`: ids never fall; every page has 1 to 8 blocks and one has exactly 8. `ref_group`: a row's 4 values differ; the rows of the 16 blocks of one ctx group name every ctx group exactly 4 times.
All inputs are finite; a program needn't handle non-finite values.
Results may differ from the reference program's by a relative error of at most 0.0042.
Values may be sent and summed in bfloat16 or wider, within the bound.
No kernel may reach another device: no remote copies, remote signals or barrier semaphores. Data moves between devices by JAX's collectives and lax.ppermute only.
A program may use at most 128 MiB of HBM per device.

```python
import math
import jax
import jax.numpy as jnp
import numpy as np
from jax import lax

HEADS = 64
KV_HEADS = 8
HD = 128
BLOCK = 128
MAXPAGE = 8
REFS = 4
QB = 16
NB = 256
TOKENS = 32768
CAP = 4
PAGES = 64
N_CTX = 16


def drawn_pair(key):
    base_key = jax.random.fold_in(key, 1117)
    keys_raw = jnp.clip(jax.random.normal(jax.random.fold_in(base_key, 1), (TOKENS, KV_HEADS * HD), jnp.float32), -4.5, 4.5)
    query_raw = jnp.clip(jax.random.normal(jax.random.fold_in(base_key, 2), (TOKENS, HEADS * HD), jnp.float32), -4.5, 4.5)
    keys_out = keys_raw
    query_out = query_raw
    return (query_out, keys_out)


def draw_queries(key, part):
    return drawn_pair(key)[0].astype(jnp.bfloat16)


def draw_key_states(key, part):
    return drawn_pair(key)[1].astype(jnp.bfloat16)


def touch_ends(drawn, stream_key, smallest, high):
    place = [jax.random.randint(jax.random.fold_in(stream_key, axis), (), 0, length) for axis, length in enumerate(drawn.shape)]
    longest = drawn.shape.index(max(drawn.shape))
    neighbour = place[:longest] + [(place[longest] + 1) % drawn.shape[longest]] + place[longest + 1:]
    return drawn.at[tuple(place)].set(smallest).at[tuple(neighbour)].set(high)


def level_of(rng, shape, shards, low, largest):
    factor_of = 1.0
    for dim, blocks in shards:
        heights = jax.random.uniform(jax.random.fold_in(jax.random.fold_in(rng, 6), dim), (blocks,), jnp.float32, low / len(shards), largest / len(shards))
        factor_of = factor_of * jnp.repeat(jnp.exp(heights), shape[dim] // blocks).reshape((-1,) + (1,) * (len(shape) - 1 - dim))
    return factor_of


def split_up(amount, total, bound, slope):
    portions = [(1 << 20) // math.isqrt(grade ** slope) + 1 for grade in range(2, amount + 1)]
    spare, counts = total - bound - (amount - 1), [1] * (amount - 1)
    while spare > 0:
        free = [i for i in range(amount - 1) if counts[i] < bound]
        mass, budget = sum([portions[i] for i in free]), spare
        for i in free:
            addition = min(bound - counts[i], max(1, budget * portions[i] // mass), spare)
            counts[i] = counts[i] + addition
            spare = spare - addition
    return np.array([bound] + counts)


def uneven(rng, amount, total, most, lean):
    if amount == 2:
        one = jax.random.randint(rng, (), max(1, total - most), min(most, total - 1) + 1)
        return jnp.stack([one, total - one])
    tallies = jnp.asarray(split_up(amount, total, most, lean), jnp.int32)
    pairs = (amount - 1) // 2
    donor, receiver = tallies[1:1 + 2 * pairs:2], tallies[2:2 + 2 * pairs:2]
    margin = jnp.minimum(donor - 1, most - receiver)
    moved = jax.random.randint(jax.random.fold_in(rng, 1), (pairs,), 0, 1 << 20) % (margin + 1)
    tallies = tallies.at[1:1 + 2 * pairs:2].set(donor - moved).at[2:2 + 2 * pairs:2].set(receiver + moved)
    return tallies[jax.random.permutation(jax.random.fold_in(rng, 2), amount)]


def deal_out(key, own, number, rows, amount, top, most, lean):
    sequence = jax.random.permutation(key, amount)
    crowded, ordinary = load_shares(amount, rows * top, most, lean, True), load_shares(amount, rows * top, most, lean, False)
    places = jnp.arange(amount)

    def named(sizes, offset_by):
        used = int((sizes > 0).sum())
        fixed = max(1, used // 4)
        passed = fixed + (places - fixed + offset_by * (used - fixed)) % max(1, amount - fixed)
        return jnp.zeros((amount,), jnp.int32).at[sequence[jnp.where(places < fixed, places, passed)]].set(jnp.asarray(sizes, jnp.int32))

    sizes = jnp.where(number % 4 == 0, named(crowded, number // 4), named(ordinary, number - number // 4 - 1))
    mixed = jax.random.permutation(jax.random.fold_in(own, 3), amount)
    donor, sink = mixed[0:amount // 2 * 2:2], mixed[1:amount // 2 * 2:2]
    room = jnp.minimum(sizes[donor] - 1, most - sizes[sink]) // 2
    room = jnp.where((donor == sequence[0]) | (sink == sequence[0]) | (sizes[sink] == 0), 0, jnp.maximum(room, 0))
    passed = jax.random.randint(jax.random.fold_in(own, 4), (amount // 2,), 0, 1 << 20) % (room + 1)
    sizes = sizes.at[donor].add(-passed).at[sink].add(passed)
    items = jnp.searchsorted(jnp.cumsum(sizes), jnp.arange(rows * top), side="right").astype(jnp.int32)
    table = items.reshape(top, rows).T
    table = table[jax.random.permutation(jax.random.fold_in(own, 1), rows)]
    offset_by = jax.random.randint(jax.random.fold_in(own, 2), (rows, 1), 0, top)
    return jnp.take_along_axis(table, (jnp.arange(top)[None, :] + offset_by) % top, axis=1)


def load_shares(number_of, total, most, lean, full):
    weights = [(1 << 20) // math.isqrt(grade ** lean) + 1 for grade in range(1, number_of + 1)]
    largest = most if full else min(most, max(-(-total // number_of), total * weights[0] // sum(weights)))
    least = 1 if total - largest >= number_of - 1 else 0
    given, rest = [largest] + [least] * (number_of - 1), total - largest - least * (number_of - 1)
    while rest > 0:
        movable = [i for i in range(1, number_of) if given[i] < largest] or [i for i in range(1, number_of) if given[i] < most]
        mass, remaining = sum([weights[i] for i in movable]), rest
        for i in movable:
            addition = min(most - given[i], max(1, remaining * weights[i] // mass), rest)
            given[i] = given[i] + addition
            rest = rest - addition
    return np.array(given)


def scatter_about(own_key, extent, width, most, split=(), kind=jnp.bfloat16):
    drawn = width * jax.random.normal(own_key, extent, jnp.float32)
    if split:
        drawn = drawn * level_of(own_key, extent, split, -0.22, 0.18)
    return jnp.clip(drawn, -most, most).astype(kind)


def setup_inputs(seed: int = 0) -> dict:
    seeds = jax.random.split(jax.random.key(seed), 7)
    queries = draw_queries(jax.random.fold_in(seeds[6], 71), 0)
    key_states = draw_key_states(jax.random.fold_in(seeds[6], 71), 0)
    value_states = scatter_about(seeds[2], (TOKENS, KV_HEADS * HD), 1.0, 6.0, ((0, 128),))
    page_ids = jnp.searchsorted(jnp.cumsum(uneven(seeds[3], PAGES, NB, MAXPAGE, 2)), jnp.arange(NB), side="right").astype(jnp.int32)
    ref_group_keys = jax.random.split(jax.random.fold_in(seeds[4], 1), NB // QB)
    ref_group_turns = jax.random.permutation(jax.random.fold_in(seeds[4], 3), NB // QB)
    ref_group = jax.vmap(lambda own, number: deal_out(jax.random.fold_in(seeds[4], 2), own, number, QB, N_CTX, REFS, CAP, 2))(ref_group_keys, ref_group_turns).reshape((NB, REFS))
    ref_slot = touch_ends(jax.random.randint(seeds[5], (NB, REFS), 0, QB), jax.random.fold_in(seeds[5], 1), 0, QB - 1).astype(jnp.int32)
    return dict(queries=queries, key_states=key_states, value_states=value_states, page_ids=page_ids, ref_group=ref_group, ref_slot=ref_slot)


def page_starts(page_ids):
    block_count = page_ids.shape[0]
    position = jnp.arange(block_count, dtype=jnp.int32)
    is_fresh = jnp.concatenate([jnp.ones((1,), dtype=jnp.bool_), page_ids[1:] != page_ids[:-1]])
    return lax.cummax(jnp.where(is_fresh, position, jnp.zeros_like(position)), axis=0)

def allowed_mask(global_block, padded_pages, starts, ref_row, block_size, window):
    nearby = lax.dynamic_slice_in_dim(padded_pages, global_block, window, 0)
    own_page = nearby[window - 1]
    inside = nearby == own_page
    offsets = jnp.arange(window)
    is_last = offsets == window - 1
    rows_at = jnp.arange(block_size)
    causal = rows_at[None, :] <= rows_at[:, None]
    window_ok = inside[None, :, None] & (jnp.logical_not(is_last)[None, :, None] | causal[:, None, :])
    window_ok = window_ok.reshape(block_size, window * block_size)
    start_here = lax.dynamic_index_in_dim(starts, global_block, 0, keepdims=False)
    ref_ok = ref_row < start_here
    ref_ok = jnp.broadcast_to(ref_ok[None, :, None], (block_size, ref_row.shape[0], block_size))
    return jnp.concatenate([window_ok, ref_ok.reshape(block_size, -1)], axis=1)

def attend(query_block, key_set, value_set, allowed):
    score_scale = 1.0 / math.sqrt(query_block.shape[-1])
    scores = jnp.einsum('tgqd,sgd->gqts', query_block.astype(jnp.float32), key_set.astype(jnp.float32)) * score_scale
    scores = jnp.where(allowed, scores, -1e+30)
    row_max = lax.optimization_barrier(jnp.max(scores, axis=-1, keepdims=True))
    exp_scores = jnp.where(allowed, jnp.exp(scores - row_max), 0.0)
    totals = lax.optimization_barrier(jnp.sum(exp_scores, axis=-1))
    weights = lax.optimization_barrier(exp_scores.astype(jnp.bfloat16))
    mixture = jnp.einsum('gqts,sgd->tgqd', weights.astype(jnp.float32), value_set.astype(jnp.float32))
    return (mixture / jnp.transpose(totals, (2, 0, 1))[..., None]).astype(jnp.bfloat16)

def reference(queries, key_states, value_states, page_ids, ref_group, ref_slot):
    token_count = queries.shape[0]
    block_count = token_count // BLOCK
    group_size = HEADS // KV_HEADS
    reach = MAXPAGE - 1
    query_blocks = queries.reshape(block_count, BLOCK, KV_HEADS, group_size, HD)
    key_blocks = key_states.reshape(block_count, BLOCK, KV_HEADS, HD)
    value_blocks = value_states.reshape(block_count, BLOCK, KV_HEADS, HD)
    pad_keys = jnp.concatenate([jnp.zeros((reach, BLOCK, KV_HEADS, HD), key_states.dtype), key_blocks])
    pad_values = jnp.concatenate([jnp.zeros((reach, BLOCK, KV_HEADS, HD), value_states.dtype), value_blocks])
    page_table = page_ids.astype(jnp.int32)
    padded_pages = jnp.concatenate([jnp.full((reach,), -1, dtype=jnp.int32), page_table])
    starts = page_starts(page_table)
    ref_rows = (ref_group * QB + ref_slot).astype(jnp.int32)

    def one_block(global_block):
        ref_row = lax.dynamic_index_in_dim(ref_rows, global_block, 0, keepdims=False)
        near_keys = lax.dynamic_slice_in_dim(pad_keys, global_block, MAXPAGE, 0)
        near_values = lax.dynamic_slice_in_dim(pad_values, global_block, MAXPAGE, 0)
        far_keys = jnp.take(key_blocks, ref_row, axis=0)
        far_values = jnp.take(value_blocks, ref_row, axis=0)
        key_set = jnp.concatenate([near_keys, far_keys]).reshape(-1, KV_HEADS, HD)
        value_set = jnp.concatenate([near_values, far_values]).reshape(-1, KV_HEADS, HD)
        allowed = allowed_mask(global_block, padded_pages, starts, ref_row, BLOCK, MAXPAGE)
        query_block = lax.dynamic_index_in_dim(query_blocks, global_block, 0, keepdims=False)
        return attend(query_block, key_set, value_set, allowed)
    outputs = lax.map(one_block, jnp.arange(block_count, dtype=jnp.int32))
    return outputs.reshape(token_count, HEADS * HD)
```

```python
import functools
import math

import jax
import jax.numpy as jnp
from jax import lax
from jax.experimental import pallas as pl
from jax.experimental.pallas import tpu as pltpu
from jax.sharding import PartitionSpec as P

HD = 128
BLOCK = 128
MAXPAGE = 8
TAIL = MAXPAGE - 1


def page_starts(page_ids):
    block_count = page_ids.shape[0]
    position = jnp.arange(block_count, dtype=jnp.int32)
    is_fresh = jnp.concatenate([jnp.ones((1,), dtype=jnp.bool_), page_ids[1:] != page_ids[:-1]])
    return lax.cummax(jnp.where(is_fresh, position, jnp.zeros_like(position)), axis=0)


def attn_kernel(kidx_ref, cnt_ref, q_ref, k_ref, v_ref, o_ref, s_scr, m_scr, l_scr, acc_scr, *, scale, group):
    i = pl.program_id(0)
    n = cnt_ref[i]
    diag = TAIL + i
    rows = q_ref.shape[1] * BLOCK
    q = q_ref[0, :, 0].reshape(rows, HD)
    tok = lax.broadcasted_iota(jnp.int32, (rows, BLOCK), 0) % BLOCK
    ahead = lax.broadcasted_iota(jnp.int32, (rows, BLOCK), 1) - tok
    m_scr[...] = jnp.full(m_scr.shape, -1e30, jnp.float32)

    def scores(t, carry):
        kb = kidx_ref[i, t]
        s = lax.dot_general(
            q, k_ref[kb], (((1,), (1,)), ((), ())), preferred_element_type=jnp.float32
        ) * scale
        limit = jnp.where(kb == diag, 0, BLOCK)
        s = jnp.where(ahead <= limit, s, -1e30)
        s_scr[t] = s
        m_scr[...] = jnp.maximum(m_scr[...], s)
        return carry

    lax.fori_loop(0, n, scores, 0)
    m = jnp.max(m_scr[...], axis=1, keepdims=True)
    l_scr[...] = jnp.zeros(l_scr.shape, jnp.float32)
    acc_scr[...] = jnp.zeros(acc_scr.shape, jnp.float32)

    def mix(t, carry):
        kb = kidx_ref[i, t]
        p = jnp.exp(s_scr[t] - m)
        l_scr[...] += p
        acc_scr[...] += jnp.dot(p.astype(jnp.bfloat16), v_ref[kb], preferred_element_type=jnp.float32)
        return carry

    lax.fori_loop(0, n, mix, 0)
    total = jnp.sum(l_scr[...], axis=1, keepdims=True)
    out = acc_scr[...] / total
    o_ref[0, :, 0] = out.reshape(group, BLOCK, HD).astype(o_ref.dtype)


def attention(kidx, cnt, q5, k_all, v_all):
    src, group, halves = q5.shape[0], q5.shape[1], q5.shape[2]
    blocks = src * halves
    nk = k_all.shape[0]
    width = kidx.shape[1]
    rows = group * BLOCK
    q_spec = pl.BlockSpec((1, group, 1, BLOCK, HD), lambda i, kidx, cnt: (i // halves, 0, i % halves, 0, 0))
    kv_spec = pl.BlockSpec((nk, BLOCK, HD), lambda i, kidx, cnt: (0, 0, 0))
    flops = 4 * blocks * 6 * rows * BLOCK * HD
    cost = pl.CostEstimate(
        flops=flops,
        transcendentals=blocks * 6 * rows * BLOCK,
        bytes_accessed=2 * q5.size * 2 + 2 * k_all.size * 2,
    )
    return pl.pallas_call(
        functools.partial(attn_kernel, scale=1.0 / math.sqrt(HD), group=group),
        out_shape=jax.ShapeDtypeStruct(q5.shape, q5.dtype),
        grid_spec=pltpu.PrefetchScalarGridSpec(
            num_scalar_prefetch=2,
            grid=(blocks,),
            in_specs=[q_spec, kv_spec, kv_spec],
            out_specs=q_spec,
            scratch_shapes=[
                pltpu.VMEM((width, rows, BLOCK), jnp.float32),
                pltpu.VMEM((rows, BLOCK), jnp.float32),
                pltpu.VMEM((rows, BLOCK), jnp.float32),
                pltpu.VMEM((rows, HD), jnp.float32),
            ],
        ),
        compiler_params=pltpu.CompilerParams(
            dimension_semantics=("arbitrary",), vmem_limit_bytes=48 * 1024 * 1024
        ),
        cost_estimate=cost,
    )(kidx, cnt, q5, k_all, v_all)


def shards(queries, key_states, value_states, page_ids, ref_group, ref_slot):
    n_head = lax.axis_size("head")
    n_ctx = lax.axis_size("ctx")
    tokens = queries.shape[0]
    kv_width = key_states.shape[1]
    kv_heads = kv_width // HD
    group = queries.shape[1] // kv_width
    halves = tokens // BLOCK
    blocks = n_head * halves
    refs = ref_group.shape[1]
    cap = blocks * refs // n_ctx

    q4 = queries.reshape(tokens, kv_heads, group, HD).transpose(1, 2, 0, 3)
    kv4 = jnp.stack(
        [
            key_states.reshape(tokens, kv_heads, HD).transpose(1, 0, 2),
            value_states.reshape(tokens, kv_heads, HD).transpose(1, 0, 2),
        ],
        axis=1,
    )
    kv_here = lax.all_to_all(kv4, "head", split_axis=0, concat_axis=0, tiled=True)
    q_here = lax.all_to_all(q4, "head", split_axis=0, concat_axis=0, tiled=True)
    own_k = kv_here[:, 0].reshape(blocks, BLOCK, HD)
    own_v = kv_here[:, 1].reshape(blocks, BLOCK, HD)
    own_kv = jnp.stack([own_k, own_v], axis=1)

    devices = range(n_ctx)
    route = [(i - 1, i) for i in devices if i - 1 in devices]
    tail_kv = lax.ppermute(own_kv[blocks - TAIL:], "ctx", route)

    me = lax.axis_index("ctx")
    rg = ref_group.reshape(n_ctx, blocks * refs)
    rs = ref_slot.reshape(n_ctx, blocks * refs)
    hit = (rg[:, :, None] == jnp.arange(n_ctx, dtype=jnp.int32)[None, None, :]).astype(jnp.int32)
    rank = jnp.sum((jnp.cumsum(hit, axis=1) - 1) * hit, axis=2)
    pick = (rg == me)[:, :, None] & (rank[:, :, None] == jnp.arange(cap, dtype=jnp.int32)[None, None, :])
    send_idx = jnp.sum(jnp.where(pick, rs[:, :, None], 0), axis=1)
    send_kv = jnp.take(own_kv, send_idx.reshape(-1), axis=0).reshape(n_ctx, cap, 2, BLOCK, HD)
    recv_kv = lax.all_to_all(send_kv, "ctx", split_axis=0, concat_axis=0, tiled=True)
    recv_kv = recv_kv.reshape(n_ctx * cap, 2, BLOCK, HD)

    all_kv = jnp.concatenate([tail_kv, own_kv, recv_kv], axis=0)
    k_all = all_kv[:, 0]
    v_all = all_kv[:, 1]

    starts = page_starts(page_ids)
    first = me * blocks
    local = jnp.arange(blocks, dtype=jnp.int32)
    gblock = first + local
    st = lax.dynamic_slice_in_dim(starts, first, blocks, 0)
    near_t = jnp.arange(MAXPAGE, dtype=jnp.int32)
    near_ok = near_t[None, :] <= (gblock - st)[:, None]
    near_idx = (st - first + TAIL)[:, None] + near_t[None, :]
    my_rg = lax.dynamic_slice_in_dim(ref_group, first, blocks, 0)
    my_rs = lax.dynamic_slice_in_dim(ref_slot, first, blocks, 0)
    my_rank = lax.dynamic_index_in_dim(rank, me, 0, keepdims=False).reshape(blocks, refs)
    ref_ok = (my_rg * blocks + my_rs) < st[:, None]
    ref_idx = TAIL + blocks + my_rg * cap + my_rank
    cand = jnp.concatenate([near_idx, ref_idx], axis=1)
    ok = jnp.concatenate([near_ok, ref_ok], axis=1)
    pos = jnp.cumsum(ok.astype(jnp.int32), axis=1) - 1
    width = MAXPAGE + refs
    slot = jnp.arange(width, dtype=jnp.int32)
    place = ok[:, :, None] & (pos[:, :, None] == slot[None, None, :])
    kidx = jnp.sum(jnp.where(place, cand[:, :, None], 0), axis=1).astype(jnp.int32)
    cnt = jnp.sum(ok.astype(jnp.int32), axis=1).astype(jnp.int32)

    q5 = q_here.reshape(n_head, group, halves, BLOCK, HD)
    out5 = attention(kidx, cnt, q5, k_all, v_all)
    out4 = out5.reshape(n_head, group, tokens, HD)
    back = lax.all_to_all(out4, "head", split_axis=0, concat_axis=0, tiled=True)
    return back.transpose(2, 0, 1, 3).reshape(tokens, kv_heads * group * HD)


def solution(mesh):
    placed = (
        P(("ctx", "head"), None),
        P(("ctx", "head"), None),
        P(("ctx", "head"), None),
        P(),
        P(),
        P(),
    )
    return jax.shard_map(
        shards, mesh=mesh, in_specs=placed, out_specs=P(("ctx", "head"), None), check_vma=False
    )
```

```python
import functools
import math

import jax
import jax.numpy as jnp
from jax import lax
from jax.experimental import pallas as pl
from jax.experimental.pallas import tpu as pltpu
from jax.sharding import PartitionSpec as P

HD = 128
BLOCK = 128
MAXPAGE = 8
TAIL = MAXPAGE - 1


def page_starts(page_ids):
    block_count = page_ids.shape[0]
    position = jnp.arange(block_count, dtype=jnp.int32)
    is_fresh = jnp.concatenate([jnp.ones((1,), dtype=jnp.bool_), page_ids[1:] != page_ids[:-1]])
    return lax.cummax(jnp.where(is_fresh, position, jnp.zeros_like(position)), axis=0)


def attn_kernel(kidx_ref, cnt_ref, q_ref, kv_ref, o_ref, s_scr, m_scr, l_scr, acc_scr, *, scale, group, half):
    j = pl.program_id(0)
    b = j * 2 + half
    n = cnt_ref[b]
    diag = TAIL + b
    rows = group * BLOCK
    q_tile = q_ref[0]
    q = jnp.concatenate([q_tile[:, h * HD:(h + 1) * HD] for h in range(group)], axis=0)
    tok = lax.broadcasted_iota(jnp.int32, (rows, BLOCK), 0) % BLOCK
    ahead = lax.broadcasted_iota(jnp.int32, (rows, BLOCK), 1) - tok
    m_scr[...] = jnp.full(m_scr.shape, -1e30, jnp.float32)

    def scores(t, carry):
        kb = kidx_ref[b, t]
        s = lax.dot_general(
            q, kv_ref[kb, 0], (((1,), (1,)), ((), ())), preferred_element_type=jnp.float32
        ) * scale
        limit = jnp.where(kb == diag, 0, BLOCK)
        s = jnp.where(ahead <= limit, s, -1e30)
        s_scr[t] = s
        m_scr[...] = jnp.maximum(m_scr[...], s)
        return carry

    lax.fori_loop(0, n, scores, 0)
    m = jnp.max(m_scr[...], axis=1, keepdims=True)
    l_scr[...] = jnp.zeros(l_scr.shape, jnp.float32)
    acc_scr[...] = jnp.zeros(acc_scr.shape, jnp.float32)

    def mix(t, carry):
        kb = kidx_ref[b, t]
        p = jnp.exp(s_scr[t] - m)
        l_scr[...] += p
        acc_scr[...] += jnp.dot(p.astype(jnp.bfloat16), kv_ref[kb, 1], preferred_element_type=jnp.float32)
        return carry

    lax.fori_loop(0, n, mix, 0)
    total = jnp.sum(l_scr[...], axis=1, keepdims=True)
    out = acc_scr[...] / total
    for h in range(group):
        o_ref[0, :, h * HD:(h + 1) * HD] = out[h * BLOCK:(h + 1) * BLOCK].astype(o_ref.dtype)


def attention(kidx, cnt, q3, all_kv, half):
    src, width_q = q3.shape[0], q3.shape[2]
    group = width_q // HD
    nk = all_kv.shape[0]
    width = kidx.shape[1]
    rows = group * BLOCK
    q_spec = pl.BlockSpec((1, BLOCK, width_q), lambda j, kidx, cnt: (j, 0, 0))
    kv_spec = pl.BlockSpec((nk, 2, BLOCK, HD), lambda j, kidx, cnt: (0, 0, 0, 0))
    cost = pl.CostEstimate(
        flops=4 * src * 6 * rows * BLOCK * HD,
        transcendentals=src * 6 * rows * BLOCK,
        bytes_accessed=2 * q3.size * 2 + all_kv.size * 2,
    )
    return pl.pallas_call(
        functools.partial(attn_kernel, scale=1.0 / math.sqrt(HD), group=group, half=half),
        out_shape=jax.ShapeDtypeStruct(q3.shape, q3.dtype),
        grid_spec=pltpu.PrefetchScalarGridSpec(
            num_scalar_prefetch=2,
            grid=(src,),
            in_specs=[q_spec, kv_spec],
            out_specs=q_spec,
            scratch_shapes=[
                pltpu.VMEM((width, rows, BLOCK), jnp.float32),
                pltpu.VMEM((rows, BLOCK), jnp.float32),
                pltpu.VMEM((rows, BLOCK), jnp.float32),
                pltpu.VMEM((rows, HD), jnp.float32),
            ],
        ),
        compiler_params=pltpu.CompilerParams(
            dimension_semantics=("arbitrary",), vmem_limit_bytes=48 * 1024 * 1024
        ),
        cost_estimate=cost,
    )(kidx, cnt, q3, all_kv)


def shards(queries, key_states, value_states, page_ids, ref_group, ref_slot):
    n_head = lax.axis_size("head")
    n_ctx = lax.axis_size("ctx")
    tokens = queries.shape[0]
    kv_width = key_states.shape[1]
    kv_heads = kv_width // HD
    q_width = queries.shape[1] // kv_heads
    halves = tokens // BLOCK
    blocks = n_head * halves
    refs = ref_group.shape[1]
    cap = blocks * refs // n_ctx

    kv4 = jnp.stack(
        [
            key_states.reshape(tokens, kv_heads, HD).transpose(1, 0, 2),
            value_states.reshape(tokens, kv_heads, HD).transpose(1, 0, 2),
        ],
        axis=1,
    )
    kv_here = lax.all_to_all(kv4, "head", split_axis=0, concat_axis=0, tiled=True)
    own_kv = (
        kv_here.reshape(n_head, 2, halves, BLOCK, HD).transpose(0, 2, 1, 3, 4).reshape(blocks, 2, BLOCK, HD)
    )

    q_t = queries.reshape(halves, BLOCK, kv_heads, q_width).transpose(0, 2, 1, 3)
    q_parts = [
        lax.all_to_all(q_t[h], "head", split_axis=0, concat_axis=0, tiled=True) for h in range(halves)
    ]

    me = lax.axis_index("ctx")
    rg = ref_group.reshape(n_ctx, blocks * refs)
    rs = ref_slot.reshape(n_ctx, blocks * refs)
    hit = (rg[:, :, None] == jnp.arange(n_ctx, dtype=jnp.int32)[None, None, :]).astype(jnp.int32)
    rank = jnp.sum((jnp.cumsum(hit, axis=1) - 1) * hit, axis=2)
    pick = (rg == me)[:, :, None] & (rank[:, :, None] == jnp.arange(cap, dtype=jnp.int32)[None, None, :])
    send_idx = jnp.sum(jnp.where(pick, rs[:, :, None], 0), axis=1)
    shift = jnp.arange(n_ctx, dtype=jnp.int32)
    send_rolled = jnp.take(send_idx, (me + shift) % n_ctx, axis=0)
    send_kv = jnp.take(own_kv, send_rolled.reshape(-1), axis=0).reshape(n_ctx, cap, 2, BLOCK, HD)
    pieces = []
    for k in range(1, n_ctx):
        route = [(g, g + k) for g in range(n_ctx - k)]
        if k == 1:
            payload = jnp.concatenate([own_kv[blocks - TAIL:], send_kv[1]], axis=0)
            got = lax.ppermute(payload, "ctx", route)
            tail_kv = got[:TAIL]
            pieces.append(got[TAIL:])
        else:
            pieces.append(lax.ppermute(send_kv[k], "ctx", route))
    all_kv = jnp.concatenate([tail_kv, own_kv, send_kv[0]] + pieces, axis=0)

    starts = page_starts(page_ids)
    first = me * blocks
    local = jnp.arange(blocks, dtype=jnp.int32)
    gblock = first + local
    st = lax.dynamic_slice_in_dim(starts, first, blocks, 0)
    near_t = jnp.arange(MAXPAGE, dtype=jnp.int32)
    near_ok = near_t[None, :] <= (gblock - st)[:, None]
    near_idx = (st - first + TAIL)[:, None] + near_t[None, :]
    my_rg = lax.dynamic_slice_in_dim(ref_group, first, blocks, 0)
    my_rs = lax.dynamic_slice_in_dim(ref_slot, first, blocks, 0)
    my_rank = lax.dynamic_index_in_dim(rank, me, 0, keepdims=False).reshape(blocks, refs)
    ref_ok = ((my_rg * blocks + my_rs) < st[:, None]) & (my_rg <= me)
    ref_idx = TAIL + blocks + (me - my_rg) * cap + my_rank
    cand = jnp.concatenate([near_idx, ref_idx], axis=1)
    ok = jnp.concatenate([near_ok, ref_ok], axis=1)
    pos = jnp.cumsum(ok.astype(jnp.int32), axis=1) - 1
    width = MAXPAGE + refs
    slot = jnp.arange(width, dtype=jnp.int32)
    place = ok[:, :, None] & (pos[:, :, None] == slot[None, None, :])
    kidx = jnp.sum(jnp.where(place, cand[:, :, None], 0), axis=1).astype(jnp.int32)
    cnt = jnp.sum(ok.astype(jnp.int32), axis=1).astype(jnp.int32)

    outs = []
    for h in range(halves):
        out_h = attention(kidx, cnt, q_parts[h], all_kv, h)
        outs.append(lax.all_to_all(out_h, "head", split_axis=0, concat_axis=0, tiled=True))
    back = jnp.stack(outs, axis=0)
    return back.transpose(0, 2, 1, 3).reshape(tokens, kv_heads * q_width)


def solution(mesh):
    placed = (
        P(("ctx", "head"), None),
        P(("ctx", "head"), None),
        P(("ctx", "head"), None),
        P(),
        P(),
        P(),
    )
    return jax.shard_map(
        shards, mesh=mesh, in_specs=placed, out_specs=P(("ctx", "head"), None), check_vma=False
    )
```

```python
import functools
import math

import jax
import jax.numpy as jnp
from jax import lax
from jax.experimental import pallas as pl
from jax.experimental.pallas import tpu as pltpu
from jax.sharding import PartitionSpec as P

HD = 128
BLOCK = 128
MAXPAGE = 8
TAIL = MAXPAGE - 1


def page_starts(page_ids):
    block_count = page_ids.shape[0]
    position = jnp.arange(block_count, dtype=jnp.int32)
    is_fresh = jnp.concatenate([jnp.ones((1,), dtype=jnp.bool_), page_ids[1:] != page_ids[:-1]])
    return lax.cummax(jnp.where(is_fresh, position, jnp.zeros_like(position)), axis=0)


def attn_kernel(kidx_ref, cnt_ref, q_ref, *rest, scale, group, half, parts):
    kv_parts = rest[:parts]
    o_ref = rest[parts]
    kv_ref, sem, s_scr, m_scr, l_scr, acc_scr = rest[parts + 1:]
    j = pl.program_id(0)

    @pl.when(j == 0)
    def _():
        copies = []
        start = 0
        for idx, part in enumerate(kv_parts):
            size = part.shape[0]
            copy = pltpu.make_async_copy(part, kv_ref.at[pl.ds(start, size)], sem.at[idx])
            copy.start()
            copies.append(copy)
            start += size
        for copy in copies:
            copy.wait()

    b = j * 2 + half
    n = cnt_ref[b]
    diag = TAIL + b
    rows = group * BLOCK
    q_tile = q_ref[0]
    q = jnp.concatenate([q_tile[:, h * HD:(h + 1) * HD] for h in range(group)], axis=0)
    tok = lax.broadcasted_iota(jnp.int32, (rows, BLOCK), 0) % BLOCK
    ahead = lax.broadcasted_iota(jnp.int32, (rows, BLOCK), 1) - tok
    m_scr[...] = jnp.full(m_scr.shape, -1e30, jnp.float32)

    def scores(t, carry):
        kb = kidx_ref[b, t]
        s = lax.dot_general(
            q, kv_ref[kb, 0], (((1,), (1,)), ((), ())), preferred_element_type=jnp.float32
        ) * scale
        limit = jnp.where(kb == diag, 0, BLOCK)
        s = jnp.where(ahead <= limit, s, -1e30)
        s_scr[t] = s
        m_scr[...] = jnp.maximum(m_scr[...], s)
        return carry

    lax.fori_loop(0, n, scores, 0)
    m = jnp.max(m_scr[...], axis=1, keepdims=True)
    l_scr[...] = jnp.zeros(l_scr.shape, jnp.float32)
    acc_scr[...] = jnp.zeros(acc_scr.shape, jnp.float32)

    def mix(t, carry):
        kb = kidx_ref[b, t]
        p = jnp.exp(s_scr[t] - m)
        l_scr[...] += p
        acc_scr[...] += jnp.dot(p.astype(jnp.bfloat16), kv_ref[kb, 1], preferred_element_type=jnp.float32)
        return carry

    lax.fori_loop(0, n, mix, 0)
    total = jnp.sum(l_scr[...], axis=1, keepdims=True)
    out = acc_scr[...] / total
    for h in range(group):
        o_ref[0, :, h * HD:(h + 1) * HD] = out[h * BLOCK:(h + 1) * BLOCK].astype(o_ref.dtype)


def attention(kidx, cnt, q3, kv_parts, half):
    src, width_q = q3.shape[0], q3.shape[2]
    group = width_q // HD
    nk = sum(part.shape[0] for part in kv_parts)
    width = kidx.shape[1]
    rows = group * BLOCK
    q_spec = pl.BlockSpec((1, BLOCK, width_q), lambda j, kidx, cnt: (j, 0, 0))
    any_spec = pl.BlockSpec(memory_space=pl.ANY)
    cost = pl.CostEstimate(
        flops=4 * src * 6 * rows * BLOCK * HD,
        transcendentals=src * 6 * rows * BLOCK,
        bytes_accessed=2 * q3.size * 2 + nk * 2 * BLOCK * HD * 2,
    )
    return pl.pallas_call(
        functools.partial(
            attn_kernel, scale=1.0 / math.sqrt(HD), group=group, half=half, parts=len(kv_parts)
        ),
        out_shape=jax.ShapeDtypeStruct(q3.shape, q3.dtype),
        grid_spec=pltpu.PrefetchScalarGridSpec(
            num_scalar_prefetch=2,
            grid=(src,),
            in_specs=[q_spec] + [any_spec] * len(kv_parts),
            out_specs=q_spec,
            scratch_shapes=[
                pltpu.VMEM((nk, 2, BLOCK, HD), jnp.bfloat16),
                pltpu.SemaphoreType.DMA((len(kv_parts),)),
                pltpu.VMEM((width, rows, BLOCK), jnp.float32),
                pltpu.VMEM((rows, BLOCK), jnp.float32),
                pltpu.VMEM((rows, BLOCK), jnp.float32),
                pltpu.VMEM((rows, HD), jnp.float32),
            ],
        ),
        compiler_params=pltpu.CompilerParams(
            dimension_semantics=("arbitrary",), vmem_limit_bytes=48 * 1024 * 1024
        ),
        cost_estimate=cost,
    )(kidx, cnt, q3, *kv_parts)


def shards(queries, key_states, value_states, page_ids, ref_group, ref_slot):
    n_head = lax.axis_size("head")
    n_ctx = lax.axis_size("ctx")
    tokens = queries.shape[0]
    kv_width = key_states.shape[1]
    kv_heads = kv_width // HD
    q_width = queries.shape[1] // kv_heads
    halves = tokens // BLOCK
    blocks = n_head * halves
    refs = ref_group.shape[1]
    cap = blocks * refs // n_ctx

    kv4 = jnp.stack(
        [
            key_states.reshape(tokens, kv_heads, HD).transpose(1, 0, 2),
            value_states.reshape(tokens, kv_heads, HD).transpose(1, 0, 2),
        ],
        axis=1,
    )
    kv_here = lax.all_to_all(kv4, "head", split_axis=0, concat_axis=0, tiled=True)
    own_kv = (
        kv_here.reshape(n_head, 2, halves, BLOCK, HD).transpose(0, 2, 1, 3, 4).reshape(blocks, 2, BLOCK, HD)
    )

    q_t = queries.reshape(halves, BLOCK, kv_heads, q_width).transpose(0, 2, 1, 3)
    q_parts = [
        lax.all_to_all(q_t[h], "head", split_axis=0, concat_axis=0, tiled=True) for h in range(halves)
    ]

    me = lax.axis_index("ctx")
    rg = ref_group.reshape(n_ctx, blocks * refs)
    rs = ref_slot.reshape(n_ctx, blocks * refs)
    hit = (rg[:, :, None] == jnp.arange(n_ctx, dtype=jnp.int32)[None, None, :]).astype(jnp.int32)
    rank = jnp.sum((jnp.cumsum(hit, axis=1) - 1) * hit, axis=2)
    pick = (rg == me)[:, :, None] & (rank[:, :, None] == jnp.arange(cap, dtype=jnp.int32)[None, None, :])
    send_idx = jnp.sum(jnp.where(pick, rs[:, :, None], 0), axis=1)
    shift = jnp.arange(n_ctx, dtype=jnp.int32)
    send_rolled = jnp.take(send_idx, (me + shift) % n_ctx, axis=0)
    send_kv = jnp.take(own_kv, send_rolled.reshape(-1), axis=0).reshape(n_ctx, cap, 2, BLOCK, HD)
    pieces = []
    for k in range(1, n_ctx):
        route = [(g, g + k) for g in range(n_ctx - k)]
        if k == 1:
            payload = jnp.concatenate([own_kv[blocks - TAIL:], send_kv[1]], axis=0)
            got = lax.ppermute(payload, "ctx", route)
            tail_kv = got[:TAIL]
            pieces.append(got[TAIL:])
        else:
            pieces.append(lax.ppermute(send_kv[k], "ctx", route))
    kv_parts = [tail_kv, own_kv, send_kv[0]] + pieces

    starts = page_starts(page_ids)
    first = me * blocks
    local = jnp.arange(blocks, dtype=jnp.int32)
    gblock = first + local
    st = lax.dynamic_slice_in_dim(starts, first, blocks, 0)
    near_t = jnp.arange(MAXPAGE, dtype=jnp.int32)
    near_ok = near_t[None, :] <= (gblock - st)[:, None]
    near_idx = (st - first + TAIL)[:, None] + near_t[None, :]
    my_rg = lax.dynamic_slice_in_dim(ref_group, first, blocks, 0)
    my_rs = lax.dynamic_slice_in_dim(ref_slot, first, blocks, 0)
    my_rank = lax.dynamic_index_in_dim(rank, me, 0, keepdims=False).reshape(blocks, refs)
    ref_ok = ((my_rg * blocks + my_rs) < st[:, None]) & (my_rg <= me)
    ref_idx = TAIL + blocks + (me - my_rg) * cap + my_rank
    cand = jnp.concatenate([near_idx, ref_idx], axis=1)
    ok = jnp.concatenate([near_ok, ref_ok], axis=1)
    pos = jnp.cumsum(ok.astype(jnp.int32), axis=1) - 1
    width = MAXPAGE + refs
    slot = jnp.arange(width, dtype=jnp.int32)
    place = ok[:, :, None] & (pos[:, :, None] == slot[None, None, :])
    kidx = jnp.sum(jnp.where(place, cand[:, :, None], 0), axis=1).astype(jnp.int32)
    cnt = jnp.sum(ok.astype(jnp.int32), axis=1).astype(jnp.int32)

    outs = []
    for h in range(halves):
        out_h = attention(kidx, cnt, q_parts[h], kv_parts, h)
        outs.append(lax.all_to_all(out_h, "head", split_axis=0, concat_axis=0, tiled=True))
    back = jnp.stack(outs, axis=0)
    return back.transpose(0, 2, 1, 3).reshape(tokens, kv_heads * q_width)


def solution(mesh):
    placed = (
        P(("ctx", "head"), None),
        P(("ctx", "head"), None),
        P(("ctx", "head"), None),
        P(),
        P(),
        P(),
    )
    return jax.shard_map(
        shards, mesh=mesh, in_specs=placed, out_specs=P(("ctx", "head"), None), check_vma=False
    )
```

```python
import functools
import math

import jax
import jax.numpy as jnp
from jax import lax
from jax.experimental import pallas as pl
from jax.experimental.pallas import tpu as pltpu
from jax.sharding import PartitionSpec as P

HD = 128
BLOCK = 128
MAXPAGE = 8
TAIL = MAXPAGE - 1


def page_starts(page_ids):
    block_count = page_ids.shape[0]
    position = jnp.arange(block_count, dtype=jnp.int32)
    is_fresh = jnp.concatenate([jnp.ones((1,), dtype=jnp.bool_), page_ids[1:] != page_ids[:-1]])
    return lax.cummax(jnp.where(is_fresh, position, jnp.zeros_like(position)), axis=0)


def attn_kernel(kidx_ref, cnt_ref, q_ref, *rest, scale, group, half, parts):
    kv_parts = rest[:parts]
    o_ref = rest[parts]
    kv_ref, sem, s_scr, m_scr, l_scr, acc_scr = rest[parts + 1:]
    j = pl.program_id(0)

    @pl.when(j == 0)
    def _():
        copies = []
        start = 0
        for idx, part in enumerate(kv_parts):
            size = part.shape[0]
            copy = pltpu.make_async_copy(part, kv_ref.at[pl.ds(start, size)], sem.at[idx])
            copy.start()
            copies.append(copy)
            start += size
        for copy in copies:
            copy.wait()

    b = j * 2 + half
    n = cnt_ref[b]
    diag = TAIL + b
    rows = group * BLOCK
    q_tile = q_ref[0]
    q = jnp.concatenate([q_tile[:, h * HD:(h + 1) * HD] for h in range(group)], axis=0)
    tok = lax.broadcasted_iota(jnp.int32, (rows, BLOCK), 0) % BLOCK
    ahead = lax.broadcasted_iota(jnp.int32, (rows, BLOCK), 1) - tok
    m_scr[...] = jnp.full(m_scr.shape, -1e30, jnp.float32)

    def scores(t, carry):
        kb = kidx_ref[b, t]
        s = lax.dot_general(
            q, kv_ref[kb, 0], (((1,), (1,)), ((), ())), preferred_element_type=jnp.float32
        ) * scale
        limit = jnp.where(kb == diag, 0, BLOCK)
        s = jnp.where(ahead <= limit, s, -1e30)
        s_scr[t] = s
        m_scr[...] = jnp.maximum(m_scr[...], s)
        return carry

    lax.fori_loop(0, n, scores, 0)
    m = jnp.max(m_scr[...], axis=1, keepdims=True)
    l_scr[...] = jnp.zeros(l_scr.shape, jnp.float32)
    acc_scr[...] = jnp.zeros(acc_scr.shape, jnp.float32)

    def mix(t, carry):
        kb = kidx_ref[b, t]
        p = jnp.exp(s_scr[t] - m)
        l_scr[...] += p
        acc_scr[...] += jnp.dot(p.astype(jnp.bfloat16), kv_ref[kb, 1], preferred_element_type=jnp.float32)
        return carry

    lax.fori_loop(0, n, mix, 0)
    total = jnp.sum(l_scr[...], axis=1, keepdims=True)
    out = acc_scr[...] / total
    for h in range(group):
        o_ref[0, :, h * HD:(h + 1) * HD] = out[h * BLOCK:(h + 1) * BLOCK].astype(o_ref.dtype)


def attention(kidx, cnt, q3, kv_parts, half):
    src, width_q = q3.shape[0], q3.shape[2]
    group = width_q // HD
    nk = sum(part.shape[0] for part in kv_parts)
    width = kidx.shape[1]
    rows = group * BLOCK
    q_spec = pl.BlockSpec((1, BLOCK, width_q), lambda j, kidx, cnt: (j, half, 0))
    o_spec = pl.BlockSpec((1, BLOCK, width_q), lambda j, kidx, cnt: (j, 0, 0))
    any_spec = pl.BlockSpec(memory_space=pl.ANY)
    cost = pl.CostEstimate(
        flops=4 * src * 6 * rows * BLOCK * HD,
        transcendentals=src * 6 * rows * BLOCK,
        bytes_accessed=q3.size * 2 + nk * 2 * BLOCK * HD * 2,
    )
    return pl.pallas_call(
        functools.partial(
            attn_kernel, scale=1.0 / math.sqrt(HD), group=group, half=half, parts=len(kv_parts)
        ),
        out_shape=jax.ShapeDtypeStruct((src, BLOCK, width_q), q3.dtype),
        grid_spec=pltpu.PrefetchScalarGridSpec(
            num_scalar_prefetch=2,
            grid=(src,),
            in_specs=[q_spec] + [any_spec] * len(kv_parts),
            out_specs=o_spec,
            scratch_shapes=[
                pltpu.VMEM((nk, 2, BLOCK, HD), jnp.bfloat16),
                pltpu.SemaphoreType.DMA((len(kv_parts),)),
                pltpu.VMEM((width, rows, BLOCK), jnp.float32),
                pltpu.VMEM((rows, BLOCK), jnp.float32),
                pltpu.VMEM((rows, BLOCK), jnp.float32),
                pltpu.VMEM((rows, HD), jnp.float32),
            ],
        ),
        compiler_params=pltpu.CompilerParams(
            dimension_semantics=("arbitrary",), vmem_limit_bytes=48 * 1024 * 1024
        ),
        cost_estimate=cost,
    )(kidx, cnt, q3, *kv_parts)


def shards(queries, key_states, value_states, page_ids, ref_group, ref_slot):
    n_head = lax.axis_size("head")
    n_ctx = lax.axis_size("ctx")
    tokens = queries.shape[0]
    kv_width = key_states.shape[1]
    kv_heads = kv_width // HD
    q_width = queries.shape[1] // kv_heads
    halves = tokens // BLOCK
    blocks = n_head * halves
    refs = ref_group.shape[1]
    cap = blocks * refs // n_ctx

    kv4 = jnp.stack(
        [
            key_states.reshape(tokens, kv_heads, HD).transpose(1, 0, 2),
            value_states.reshape(tokens, kv_heads, HD).transpose(1, 0, 2),
        ],
        axis=1,
    )
    kv_here = lax.all_to_all(kv4, "head", split_axis=0, concat_axis=0, tiled=True)
    own_kv = (
        kv_here.reshape(n_head, 2, halves, BLOCK, HD).transpose(0, 2, 1, 3, 4).reshape(blocks, 2, BLOCK, HD)
    )

    q_t = queries.reshape(tokens, kv_heads, q_width).transpose(1, 0, 2)
    q_here = lax.all_to_all(q_t, "head", split_axis=0, concat_axis=0, tiled=True)

    me = lax.axis_index("ctx")
    rg = ref_group.reshape(n_ctx, blocks * refs)
    rs = ref_slot.reshape(n_ctx, blocks * refs)
    hit = (rg[:, :, None] == jnp.arange(n_ctx, dtype=jnp.int32)[None, None, :]).astype(jnp.int32)
    rank = jnp.sum((jnp.cumsum(hit, axis=1) - 1) * hit, axis=2)
    pick = (rg == me)[:, :, None] & (rank[:, :, None] == jnp.arange(cap, dtype=jnp.int32)[None, None, :])
    send_idx = jnp.sum(jnp.where(pick, rs[:, :, None], 0), axis=1)
    shift = jnp.arange(n_ctx, dtype=jnp.int32)
    send_rolled = jnp.take(send_idx, (me + shift) % n_ctx, axis=0)
    send_kv = jnp.take(own_kv, send_rolled.reshape(-1), axis=0).reshape(n_ctx, cap, 2, BLOCK, HD)
    pieces = []
    for k in range(1, n_ctx):
        route = [(g, g + k) for g in range(n_ctx - k)]
        if k == 1:
            payload = jnp.concatenate([own_kv[blocks - TAIL:], send_kv[1]], axis=0)
            got = lax.ppermute(payload, "ctx", route)
            tail_kv = got[:TAIL]
            pieces.append(got[TAIL:])
        else:
            pieces.append(lax.ppermute(send_kv[k], "ctx", route))
    kv_parts = [tail_kv, own_kv, send_kv[0]] + pieces

    starts = page_starts(page_ids)
    first = me * blocks
    local = jnp.arange(blocks, dtype=jnp.int32)
    gblock = first + local
    st = lax.dynamic_slice_in_dim(starts, first, blocks, 0)
    near_t = jnp.arange(MAXPAGE, dtype=jnp.int32)
    near_ok = near_t[None, :] <= (gblock - st)[:, None]
    near_idx = (st - first + TAIL)[:, None] + near_t[None, :]
    my_rg = lax.dynamic_slice_in_dim(ref_group, first, blocks, 0)
    my_rs = lax.dynamic_slice_in_dim(ref_slot, first, blocks, 0)
    my_rank = lax.dynamic_index_in_dim(rank, me, 0, keepdims=False).reshape(blocks, refs)
    ref_ok = ((my_rg * blocks + my_rs) < st[:, None]) & (my_rg <= me)
    ref_idx = TAIL + blocks + (me - my_rg) * cap + my_rank
    cand = jnp.concatenate([near_idx, ref_idx], axis=1)
    ok = jnp.concatenate([near_ok, ref_ok], axis=1)
    pos = jnp.cumsum(ok.astype(jnp.int32), axis=1) - 1
    width = MAXPAGE + refs
    slot = jnp.arange(width, dtype=jnp.int32)
    place = ok[:, :, None] & (pos[:, :, None] == slot[None, None, :])
    kidx = jnp.sum(jnp.where(place, cand[:, :, None], 0), axis=1).astype(jnp.int32)
    cnt = jnp.sum(ok.astype(jnp.int32), axis=1).astype(jnp.int32)

    outs = []
    for h in range(halves):
        out_h = attention(kidx, cnt, q_here, kv_parts, h)
        outs.append(lax.all_to_all(out_h, "head", split_axis=0, concat_axis=0, tiled=True))
    back = jnp.stack(outs, axis=0)
    return back.transpose(0, 2, 1, 3).reshape(tokens, kv_heads * q_width)


def solution(mesh):
    placed = (
        P(("ctx", "head"), None),
        P(("ctx", "head"), None),
        P(("ctx", "head"), None),
        P(),
        P(),
        P(),
    )
    return jax.shard_map(
        shards, mesh=mesh, in_specs=placed, out_specs=P(("ctx", "head"), None), check_vma=False
    )
```

```python
import functools
import math

import jax
import jax.numpy as jnp
from jax import lax
from jax.experimental import pallas as pl
from jax.experimental.pallas import tpu as pltpu
from jax.sharding import PartitionSpec as P

HD = 128
BLOCK = 128
MAXPAGE = 8
TAIL = MAXPAGE - 1


def page_starts(page_ids):
    block_count = page_ids.shape[0]
    position = jnp.arange(block_count, dtype=jnp.int32)
    is_fresh = jnp.concatenate([jnp.ones((1,), dtype=jnp.bool_), page_ids[1:] != page_ids[:-1]])
    return lax.cummax(jnp.where(is_fresh, position, jnp.zeros_like(position)), axis=0)


def attn_kernel(kidx_ref, cnt_ref, q_ref, *rest, scale, group, half, parts):
    kv_parts = rest[:parts]
    o_ref = rest[parts]
    kv_ref, sem, s_scr, m_scr, l_scr, acc_scr = rest[parts + 1:]
    j = pl.program_id(0)

    @pl.when(j == 0)
    def _():
        copies = []
        start = 0
        for idx, part in enumerate(kv_parts):
            size = part.shape[0]
            copy = pltpu.make_async_copy(part, kv_ref.at[pl.ds(start, size)], sem.at[idx])
            copy.start()
            copies.append(copy)
            start += size
        for copy in copies:
            copy.wait()

    b = j * 2 + half
    n = cnt_ref[b]
    diag = TAIL + b
    rows = group * BLOCK
    q_tile = q_ref[0]
    q = jnp.concatenate([q_tile[:, h * HD:(h + 1) * HD] for h in range(group)], axis=0)
    tok = lax.broadcasted_iota(jnp.int32, (rows, BLOCK), 0) % BLOCK
    ahead = lax.broadcasted_iota(jnp.int32, (rows, BLOCK), 1) - tok
    m_scr[...] = jnp.full(m_scr.shape, -1e30, jnp.float32)

    def scores(t, carry):
        kb = kidx_ref[b, t]
        s = lax.dot_general(
            q, kv_ref[kb, 0], (((1,), (1,)), ((), ())), preferred_element_type=jnp.float32
        ) * scale
        limit = jnp.where(kb == diag, 0, BLOCK)
        s = jnp.where(ahead <= limit, s, -1e30)
        s_scr[t] = s
        m_scr[...] = jnp.maximum(m_scr[...], s)
        return carry

    lax.fori_loop(0, n, scores, 0)
    m = jnp.max(m_scr[...], axis=1, keepdims=True)
    l_scr[...] = jnp.zeros(l_scr.shape, jnp.float32)
    acc_scr[...] = jnp.zeros(acc_scr.shape, jnp.float32)

    def mix(t, carry):
        kb = kidx_ref[b, t]
        p = jnp.exp(s_scr[t] - m)
        l_scr[...] += p
        acc_scr[...] += jnp.dot(p.astype(jnp.bfloat16), kv_ref[kb, 1], preferred_element_type=jnp.float32)
        return carry

    lax.fori_loop(0, n, mix, 0)
    total = jnp.sum(l_scr[...], axis=1, keepdims=True)
    out = acc_scr[...] / total
    for h in range(group):
        o_ref[0, :, h * HD:(h + 1) * HD] = out[h * BLOCK:(h + 1) * BLOCK].astype(o_ref.dtype)


def attention(kidx, cnt, q3, kv_parts, half):
    src, width_q = q3.shape[0], q3.shape[2]
    group = width_q // HD
    nk = sum(part.shape[0] for part in kv_parts)
    width = kidx.shape[1]
    rows = group * BLOCK
    q_spec = pl.BlockSpec((1, BLOCK, width_q), lambda j, kidx, cnt: (j, half, 0))
    o_spec = pl.BlockSpec((1, BLOCK, width_q), lambda j, kidx, cnt: (j, 0, 0))
    any_spec = pl.BlockSpec(memory_space=pl.ANY)
    cost = pl.CostEstimate(
        flops=4 * src * 6 * rows * BLOCK * HD,
        transcendentals=src * 6 * rows * BLOCK,
        bytes_accessed=q3.size * 2 + nk * 2 * BLOCK * HD * 2,
    )
    return pl.pallas_call(
        functools.partial(
            attn_kernel, scale=1.0 / math.sqrt(HD), group=group, half=half, parts=len(kv_parts)
        ),
        out_shape=jax.ShapeDtypeStruct((src, BLOCK, width_q), q3.dtype),
        grid_spec=pltpu.PrefetchScalarGridSpec(
            num_scalar_prefetch=2,
            grid=(src,),
            in_specs=[q_spec] + [any_spec] * len(kv_parts),
            out_specs=o_spec,
            scratch_shapes=[
                pltpu.VMEM((nk, 2, BLOCK, HD), jnp.bfloat16),
                pltpu.SemaphoreType.DMA((len(kv_parts),)),
                pltpu.VMEM((width, rows, BLOCK), jnp.float32),
                pltpu.VMEM((rows, BLOCK), jnp.float32),
                pltpu.VMEM((rows, BLOCK), jnp.float32),
                pltpu.VMEM((rows, HD), jnp.float32),
            ],
        ),
        compiler_params=pltpu.CompilerParams(
            dimension_semantics=("arbitrary",), vmem_limit_bytes=48 * 1024 * 1024
        ),
        cost_estimate=cost,
    )(kidx, cnt, q3, *kv_parts)


def _copy_kernel(x_ref, o_ref):
    o_ref[...] = x_ref[...].reshape(o_ref.shape)


def split_columns(x, parts):
    rows, cols = x.shape
    width = cols // parts
    return pl.pallas_call(
        _copy_kernel,
        out_shape=jax.ShapeDtypeStruct((parts, rows, width), x.dtype),
        grid=(parts,),
        in_specs=[pl.BlockSpec((rows, width), lambda k: (0, k))],
        out_specs=pl.BlockSpec((1, rows, width), lambda k: (k, 0, 0)),
        cost_estimate=pl.CostEstimate(flops=0, transcendentals=0, bytes_accessed=2 * x.size * 2),
    )(x)


def _join_kernel(*refs):
    o_ref = refs[-1]
    rows = refs[0].shape[1]
    for h, x_ref in enumerate(refs[:-1]):
        o_ref[h * rows:(h + 1) * rows, :] = x_ref[0]


def join_columns(parts):
    count, rows, width = parts[0].shape
    total = rows * len(parts)
    return pl.pallas_call(
        _join_kernel,
        out_shape=jax.ShapeDtypeStruct((total, count * width), parts[0].dtype),
        grid=(count,),
        in_specs=[pl.BlockSpec((1, rows, width), lambda k: (k, 0, 0))] * len(parts),
        out_specs=pl.BlockSpec((total, width), lambda k: (0, k)),
        cost_estimate=pl.CostEstimate(
            flops=0, transcendentals=0, bytes_accessed=4 * parts[0].size * len(parts)
        ),
    )(*parts)


def shards(queries, key_states, value_states, page_ids, ref_group, ref_slot):
    n_head = lax.axis_size("head")
    n_ctx = lax.axis_size("ctx")
    tokens = queries.shape[0]
    kv_width = key_states.shape[1]
    kv_heads = kv_width // HD
    q_width = queries.shape[1] // kv_heads
    halves = tokens // BLOCK
    blocks = n_head * halves
    refs = ref_group.shape[1]
    cap = blocks * refs // n_ctx

    kv4 = jnp.stack(
        [
            key_states.reshape(tokens, kv_heads, HD).transpose(1, 0, 2),
            value_states.reshape(tokens, kv_heads, HD).transpose(1, 0, 2),
        ],
        axis=1,
    )
    kv_here = lax.all_to_all(kv4, "head", split_axis=0, concat_axis=0, tiled=True)
    own_kv = (
        kv_here.reshape(n_head, 2, halves, BLOCK, HD).transpose(0, 2, 1, 3, 4).reshape(blocks, 2, BLOCK, HD)
    )

    q_t = split_columns(queries, kv_heads)
    q_here = lax.all_to_all(q_t, "head", split_axis=0, concat_axis=0, tiled=True)

    me = lax.axis_index("ctx")
    rg = ref_group.reshape(n_ctx, blocks * refs)
    rs = ref_slot.reshape(n_ctx, blocks * refs)
    hit = (rg[:, :, None] == jnp.arange(n_ctx, dtype=jnp.int32)[None, None, :]).astype(jnp.int32)
    rank = jnp.sum((jnp.cumsum(hit, axis=1) - 1) * hit, axis=2)
    pick = (rg == me)[:, :, None] & (rank[:, :, None] == jnp.arange(cap, dtype=jnp.int32)[None, None, :])
    send_idx = jnp.sum(jnp.where(pick, rs[:, :, None], 0), axis=1)
    shift = jnp.arange(n_ctx, dtype=jnp.int32)
    send_rolled = jnp.take(send_idx, (me + shift) % n_ctx, axis=0)
    send_kv = jnp.take(own_kv, send_rolled.reshape(-1), axis=0).reshape(n_ctx, cap, 2, BLOCK, HD)
    pieces = []
    for k in range(1, n_ctx):
        route = [(g, g + k) for g in range(n_ctx - k)]
        if k == 1:
            payload = jnp.concatenate([own_kv[blocks - TAIL:], send_kv[1]], axis=0)
            got = lax.ppermute(payload, "ctx", route)
            tail_kv = got[:TAIL]
            pieces.append(got[TAIL:])
        else:
            pieces.append(lax.ppermute(send_kv[k], "ctx", route))
    kv_parts = [tail_kv, own_kv, send_kv[0]] + pieces

    starts = page_starts(page_ids)
    first = me * blocks
    local = jnp.arange(blocks, dtype=jnp.int32)
    gblock = first + local
    st = lax.dynamic_slice_in_dim(starts, first, blocks, 0)
    near_t = jnp.arange(MAXPAGE, dtype=jnp.int32)
    near_ok = near_t[None, :] <= (gblock - st)[:, None]
    near_idx = (st - first + TAIL)[:, None] + near_t[None, :]
    my_rg = lax.dynamic_slice_in_dim(ref_group, first, blocks, 0)
    my_rs = lax.dynamic_slice_in_dim(ref_slot, first, blocks, 0)
    my_rank = lax.dynamic_index_in_dim(rank, me, 0, keepdims=False).reshape(blocks, refs)
    ref_ok = ((my_rg * blocks + my_rs) < st[:, None]) & (my_rg <= me)
    ref_idx = TAIL + blocks + (me - my_rg) * cap + my_rank
    cand = jnp.concatenate([near_idx, ref_idx], axis=1)
    ok = jnp.concatenate([near_ok, ref_ok], axis=1)
    pos = jnp.cumsum(ok.astype(jnp.int32), axis=1) - 1
    width = MAXPAGE + refs
    slot = jnp.arange(width, dtype=jnp.int32)
    place = ok[:, :, None] & (pos[:, :, None] == slot[None, None, :])
    kidx = jnp.sum(jnp.where(place, cand[:, :, None], 0), axis=1).astype(jnp.int32)
    cnt = jnp.sum(ok.astype(jnp.int32), axis=1).astype(jnp.int32)

    outs = []
    for h in range(halves):
        out_h = attention(kidx, cnt, q_here, kv_parts, h)
        outs.append(lax.all_to_all(out_h, "head", split_axis=0, concat_axis=0, tiled=True))
    return join_columns(outs)


def solution(mesh):
    placed = (
        P(("ctx", "head"), None),
        P(("ctx", "head"), None),
        P(("ctx", "head"), None),
        P(),
        P(),
        P(),
    )
    return jax.shard_map(
        shards, mesh=mesh, in_specs=placed, out_specs=P(("ctx", "head"), None), check_vma=False
    )
```

```python
import functools
import math

import jax
import jax.numpy as jnp
from jax import lax
from jax.experimental import pallas as pl
from jax.experimental.pallas import tpu as pltpu
from jax.sharding import PartitionSpec as P

HD = 128
BLOCK = 128
MAXPAGE = 8
TAIL = MAXPAGE - 1


def page_starts(page_ids):
    block_count = page_ids.shape[0]
    position = jnp.arange(block_count, dtype=jnp.int32)
    is_fresh = jnp.concatenate([jnp.ones((1,), dtype=jnp.bool_), page_ids[1:] != page_ids[:-1]])
    return lax.cummax(jnp.where(is_fresh, position, jnp.zeros_like(position)), axis=0)


def attn_kernel(kidx_ref, cnt_ref, q_ref, *rest, scale, group, half, parts):
    kv_parts = rest[:parts]
    o_ref = rest[parts]
    kv_ref, sem, s_scr, m_scr, l_scr, acc_scr = rest[parts + 1:]
    j = pl.program_id(0)

    @pl.when(j == 0)
    def _():
        copies = []
        start = 0
        for idx, part in enumerate(kv_parts):
            size = part.shape[0]
            copy = pltpu.make_async_copy(part, kv_ref.at[pl.ds(start, size)], sem.at[idx])
            copy.start()
            copies.append(copy)
            start += size
        for copy in copies:
            copy.wait()

    b = j * 2 + half
    n = cnt_ref[b]
    diag = TAIL + b
    rows = group * BLOCK
    q_tile = q_ref[0]
    q = jnp.concatenate([q_tile[:, h * HD:(h + 1) * HD] for h in range(group)], axis=0)
    tok = lax.broadcasted_iota(jnp.int32, (rows, BLOCK), 0) % BLOCK
    ahead = lax.broadcasted_iota(jnp.int32, (rows, BLOCK), 1) - tok
    s = lax.dot_general(
        q, kv_ref[diag, 0], (((1,), (1,)), ((), ())), preferred_element_type=jnp.float32
    ) * scale
    s = jnp.where(ahead <= 0, s, -1e30)
    s_scr[0] = s
    m_scr[...] = s

    def scores(t, carry):
        kb = kidx_ref[b, t]
        s = lax.dot_general(
            q, kv_ref[kb, 0], (((1,), (1,)), ((), ())), preferred_element_type=jnp.float32
        ) * scale
        s_scr[t] = s
        m_scr[...] = jnp.maximum(m_scr[...], s)
        return carry

    lax.fori_loop(1, n, scores, 0)
    m = jnp.max(m_scr[...], axis=1, keepdims=True)
    l_scr[...] = jnp.zeros(l_scr.shape, jnp.float32)
    acc_scr[...] = jnp.zeros(acc_scr.shape, jnp.float32)

    def mix(t, carry):
        kb = kidx_ref[b, t]
        p = jnp.exp(s_scr[t] - m)
        l_scr[...] += p
        acc_scr[...] += jnp.dot(p.astype(jnp.bfloat16), kv_ref[kb, 1], preferred_element_type=jnp.float32)
        return carry

    lax.fori_loop(0, n, mix, 0)
    total = jnp.sum(l_scr[...], axis=1, keepdims=True)
    out = acc_scr[...] / total
    for h in range(group):
        o_ref[0, :, h * HD:(h + 1) * HD] = out[h * BLOCK:(h + 1) * BLOCK].astype(o_ref.dtype)


def attention(kidx, cnt, q3, kv_parts, half):
    src, width_q = q3.shape[0], q3.shape[2]
    group = width_q // HD
    nk = sum(part.shape[0] for part in kv_parts)
    width = kidx.shape[1]
    rows = group * BLOCK
    q_spec = pl.BlockSpec((1, BLOCK, width_q), lambda j, kidx, cnt: (j, half, 0))
    o_spec = pl.BlockSpec((1, BLOCK, width_q), lambda j, kidx, cnt: (j, 0, 0))
    any_spec = pl.BlockSpec(memory_space=pl.ANY)
    cost = pl.CostEstimate(
        flops=4 * src * 6 * rows * BLOCK * HD,
        transcendentals=src * 6 * rows * BLOCK,
        bytes_accessed=q3.size * 2 + nk * 2 * BLOCK * HD * 2,
    )
    return pl.pallas_call(
        functools.partial(
            attn_kernel, scale=1.0 / math.sqrt(HD), group=group, half=half, parts=len(kv_parts)
        ),
        out_shape=jax.ShapeDtypeStruct((src, BLOCK, width_q), q3.dtype),
        grid_spec=pltpu.PrefetchScalarGridSpec(
            num_scalar_prefetch=2,
            grid=(src,),
            in_specs=[q_spec] + [any_spec] * len(kv_parts),
            out_specs=o_spec,
            scratch_shapes=[
                pltpu.VMEM((nk, 2, BLOCK, HD), jnp.bfloat16),
                pltpu.SemaphoreType.DMA((len(kv_parts),)),
                pltpu.VMEM((width, rows, BLOCK), jnp.float32),
                pltpu.VMEM((rows, BLOCK), jnp.float32),
                pltpu.VMEM((rows, BLOCK), jnp.float32),
                pltpu.VMEM((rows, HD), jnp.float32),
            ],
        ),
        compiler_params=pltpu.CompilerParams(
            dimension_semantics=("arbitrary",), vmem_limit_bytes=48 * 1024 * 1024
        ),
        cost_estimate=cost,
    )(kidx, cnt, q3, *kv_parts)


def _copy_kernel(x_ref, o_ref):
    o_ref[...] = x_ref[...].reshape(o_ref.shape)


def split_columns(x, parts):
    rows, cols = x.shape
    width = cols // parts
    return pl.pallas_call(
        _copy_kernel,
        out_shape=jax.ShapeDtypeStruct((parts, rows, width), x.dtype),
        grid=(parts,),
        in_specs=[pl.BlockSpec((rows, width), lambda k: (0, k))],
        out_specs=pl.BlockSpec((1, rows, width), lambda k: (k, 0, 0)),
        cost_estimate=pl.CostEstimate(flops=0, transcendentals=0, bytes_accessed=2 * x.size * 2),
    )(x)


def _join_kernel(*refs):
    o_ref = refs[-1]
    rows = refs[0].shape[1]
    for h, x_ref in enumerate(refs[:-1]):
        o_ref[h * rows:(h + 1) * rows, :] = x_ref[0]


def join_columns(parts):
    count, rows, width = parts[0].shape
    total = rows * len(parts)
    return pl.pallas_call(
        _join_kernel,
        out_shape=jax.ShapeDtypeStruct((total, count * width), parts[0].dtype),
        grid=(count,),
        in_specs=[pl.BlockSpec((1, rows, width), lambda k: (k, 0, 0))] * len(parts),
        out_specs=pl.BlockSpec((total, width), lambda k: (0, k)),
        cost_estimate=pl.CostEstimate(
            flops=0, transcendentals=0, bytes_accessed=4 * parts[0].size * len(parts)
        ),
    )(*parts)


def shards(queries, key_states, value_states, page_ids, ref_group, ref_slot):
    n_head = lax.axis_size("head")
    n_ctx = lax.axis_size("ctx")
    tokens = queries.shape[0]
    kv_width = key_states.shape[1]
    kv_heads = kv_width // HD
    q_width = queries.shape[1] // kv_heads
    halves = tokens // BLOCK
    blocks = n_head * halves
    refs = ref_group.shape[1]
    cap = blocks * refs // n_ctx

    kv4 = jnp.stack(
        [
            key_states.reshape(tokens, kv_heads, HD).transpose(1, 0, 2),
            value_states.reshape(tokens, kv_heads, HD).transpose(1, 0, 2),
        ],
        axis=1,
    )
    kv_here = lax.all_to_all(kv4, "head", split_axis=0, concat_axis=0, tiled=True)
    own_kv = (
        kv_here.reshape(n_head, 2, halves, BLOCK, HD).transpose(0, 2, 1, 3, 4).reshape(blocks, 2, BLOCK, HD)
    )

    q_t = split_columns(queries, kv_heads)
    q_here = lax.all_to_all(q_t, "head", split_axis=0, concat_axis=0, tiled=True)

    me = lax.axis_index("ctx")
    rg = ref_group.reshape(n_ctx, blocks * refs)
    rs = ref_slot.reshape(n_ctx, blocks * refs)
    hit = (rg[:, :, None] == jnp.arange(n_ctx, dtype=jnp.int32)[None, None, :]).astype(jnp.int32)
    rank = jnp.sum((jnp.cumsum(hit, axis=1) - 1) * hit, axis=2)
    pick = (rg == me)[:, :, None] & (rank[:, :, None] == jnp.arange(cap, dtype=jnp.int32)[None, None, :])
    send_idx = jnp.sum(jnp.where(pick, rs[:, :, None], 0), axis=1)
    shift = jnp.arange(n_ctx, dtype=jnp.int32)
    send_rolled = jnp.take(send_idx, (me + shift) % n_ctx, axis=0)
    send_kv = jnp.take(own_kv, send_rolled.reshape(-1), axis=0).reshape(n_ctx, cap, 2, BLOCK, HD)
    pieces = []
    for k in range(1, n_ctx):
        route = [(g, g + k) for g in range(n_ctx - k)]
        if k == 1:
            payload = jnp.concatenate([own_kv[blocks - TAIL:], send_kv[1]], axis=0)
            got = lax.ppermute(payload, "ctx", route)
            tail_kv = got[:TAIL]
            pieces.append(got[TAIL:])
        else:
            pieces.append(lax.ppermute(send_kv[k], "ctx", route))
    kv_parts = [tail_kv, own_kv, send_kv[0]] + pieces

    starts = page_starts(page_ids)
    first = me * blocks
    local = jnp.arange(blocks, dtype=jnp.int32)
    gblock = first + local
    st = lax.dynamic_slice_in_dim(starts, first, blocks, 0)
    near_t = jnp.arange(MAXPAGE, dtype=jnp.int32)
    near_ok = (near_t[None, :] == 0) | (near_t[None, :] <= (gblock - st)[:, None])
    near_idx = jnp.where(near_t[None, :] == 0, (local + TAIL)[:, None], (st - first + TAIL - 1)[:, None] + near_t[None, :])
    my_rg = lax.dynamic_slice_in_dim(ref_group, first, blocks, 0)
    my_rs = lax.dynamic_slice_in_dim(ref_slot, first, blocks, 0)
    my_rank = lax.dynamic_index_in_dim(rank, me, 0, keepdims=False).reshape(blocks, refs)
    ref_ok = ((my_rg * blocks + my_rs) < st[:, None]) & (my_rg <= me)
    ref_idx = TAIL + blocks + (me - my_rg) * cap + my_rank
    cand = jnp.concatenate([near_idx, ref_idx], axis=1)
    ok = jnp.concatenate([near_ok, ref_ok], axis=1)
    pos = jnp.cumsum(ok.astype(jnp.int32), axis=1) - 1
    width = MAXPAGE + refs
    slot = jnp.arange(width, dtype=jnp.int32)
    place = ok[:, :, None] & (pos[:, :, None] == slot[None, None, :])
    kidx = jnp.sum(jnp.where(place, cand[:, :, None], 0), axis=1).astype(jnp.int32)
    cnt = jnp.sum(ok.astype(jnp.int32), axis=1).astype(jnp.int32)

    outs = []
    for h in range(halves):
        out_h = attention(kidx, cnt, q_here, kv_parts, h)
        outs.append(lax.all_to_all(out_h, "head", split_axis=0, concat_axis=0, tiled=True))
    return join_columns(outs)


def solution(mesh):
    placed = (
        P(("ctx", "head"), None),
        P(("ctx", "head"), None),
        P(("ctx", "head"), None),
        P(),
        P(),
        P(),
    )
    return jax.shard_map(
        shards, mesh=mesh, in_specs=placed, out_specs=P(("ctx", "head"), None), check_vma=False
    )
```

```python
import functools
import math

import jax
import jax.numpy as jnp
from jax import lax
from jax.experimental import pallas as pl
from jax.experimental.pallas import tpu as pltpu
from jax.sharding import PartitionSpec as P

HD = 128
BLOCK = 128
MAXPAGE = 8
TAIL = MAXPAGE - 1


def page_starts(page_ids):
    block_count = page_ids.shape[0]
    position = jnp.arange(block_count, dtype=jnp.int32)
    is_fresh = jnp.concatenate([jnp.ones((1,), dtype=jnp.bool_), page_ids[1:] != page_ids[:-1]])
    return lax.cummax(jnp.where(is_fresh, position, jnp.zeros_like(position)), axis=0)


def attn_kernel(kidx_ref, cnt_ref, q_ref, *rest, scale, group, half, parts):
    kv_parts = rest[:parts]
    o_ref = rest[parts]
    kv_ref, sem, s_scr, m_scr, l_scr, acc_scr = rest[parts + 1:]
    j = pl.program_id(0)

    @pl.when(j == 0)
    def _():
        copies = []
        start = 0
        for idx, part in enumerate(kv_parts):
            size = part.shape[0]
            copy = pltpu.make_async_copy(part, kv_ref.at[pl.ds(start, size)], sem.at[idx])
            copy.start()
            copies.append(copy)
            start += size
        for copy in copies:
            copy.wait()

    b = j * 2 + half
    n = cnt_ref[b]
    diag = TAIL + b
    rows = group * BLOCK
    q_tile = q_ref[0]
    q = jnp.concatenate([q_tile[:, h * HD:(h + 1) * HD] for h in range(group)], axis=0)
    tok = lax.broadcasted_iota(jnp.int32, (rows, BLOCK), 0) % BLOCK
    ahead = lax.broadcasted_iota(jnp.int32, (rows, BLOCK), 1) - tok
    dims = (((1,), (1,)), ((), ()))

    def pair(t, which):
        return jnp.concatenate(
            [kv_ref[kidx_ref[b, t], which], kv_ref[kidx_ref[b, t + 1], which]], axis=0
        )

    s = lax.dot_general(q, kv_ref[diag, 0], dims, preferred_element_type=jnp.float32) * scale
    s = jnp.where(ahead <= 0, s, -1e30)
    s_scr[0] = s
    m_scr[...] = s
    rest = n - 1
    pairs = rest // 2

    def scores(p, carry):
        t = 1 + 2 * p
        s = lax.dot_general(q, pair(t, 0), dims, preferred_element_type=jnp.float32) * scale
        s_scr[t] = s[:, :BLOCK]
        s_scr[t + 1] = s[:, BLOCK:]
        m_scr[...] = jnp.maximum(m_scr[...], jnp.maximum(s[:, :BLOCK], s[:, BLOCK:]))
        return carry

    lax.fori_loop(0, pairs, scores, 0)

    @pl.when(rest % 2 == 1)
    def _():
        t = n - 1
        s = lax.dot_general(q, kv_ref[kidx_ref[b, t], 0], dims, preferred_element_type=jnp.float32) * scale
        s_scr[t] = s
        m_scr[...] = jnp.maximum(m_scr[...], s)

    m = jnp.max(m_scr[...], axis=1, keepdims=True)

    p0 = jnp.exp(s_scr[0] - m)
    l_scr[...] = p0
    acc_scr[...] = jnp.dot(p0.astype(jnp.bfloat16), kv_ref[diag, 1], preferred_element_type=jnp.float32)

    def mix(p, carry):
        t = 1 + 2 * p
        p1 = jnp.exp(s_scr[t] - m)
        p2 = jnp.exp(s_scr[t + 1] - m)
        l_scr[...] += p1 + p2
        w = jnp.concatenate([p1, p2], axis=1).astype(jnp.bfloat16)
        acc_scr[...] += jnp.dot(w, pair(t, 1), preferred_element_type=jnp.float32)
        return carry

    lax.fori_loop(0, pairs, mix, 0)

    @pl.when(rest % 2 == 1)
    def _():
        t = n - 1
        p1 = jnp.exp(s_scr[t] - m)
        l_scr[...] += p1
        acc_scr[...] += jnp.dot(
            p1.astype(jnp.bfloat16), kv_ref[kidx_ref[b, t], 1], preferred_element_type=jnp.float32
        )

    total = jnp.sum(l_scr[...], axis=1, keepdims=True)
    out = acc_scr[...] / total
    for h in range(group):
        o_ref[0, :, h * HD:(h + 1) * HD] = out[h * BLOCK:(h + 1) * BLOCK].astype(o_ref.dtype)


def attention(kidx, cnt, q3, kv_parts, half):
    src, width_q = q3.shape[0], q3.shape[2]
    group = width_q // HD
    nk = sum(part.shape[0] for part in kv_parts)
    width = kidx.shape[1]
    rows = group * BLOCK
    q_spec = pl.BlockSpec((1, BLOCK, width_q), lambda j, kidx, cnt: (j, half, 0))
    o_spec = pl.BlockSpec((1, BLOCK, width_q), lambda j, kidx, cnt: (j, 0, 0))
    any_spec = pl.BlockSpec(memory_space=pl.ANY)
    cost = pl.CostEstimate(
        flops=4 * src * 6 * rows * BLOCK * HD,
        transcendentals=src * 6 * rows * BLOCK,
        bytes_accessed=q3.size * 2 + nk * 2 * BLOCK * HD * 2,
    )
    return pl.pallas_call(
        functools.partial(
            attn_kernel, scale=1.0 / math.sqrt(HD), group=group, half=half, parts=len(kv_parts)
        ),
        out_shape=jax.ShapeDtypeStruct((src, BLOCK, width_q), q3.dtype),
        grid_spec=pltpu.PrefetchScalarGridSpec(
            num_scalar_prefetch=2,
            grid=(src,),
            in_specs=[q_spec] + [any_spec] * len(kv_parts),
            out_specs=o_spec,
            scratch_shapes=[
                pltpu.VMEM((nk, 2, BLOCK, HD), jnp.bfloat16),
                pltpu.SemaphoreType.DMA((len(kv_parts),)),
                pltpu.VMEM((width, rows, BLOCK), jnp.float32),
                pltpu.VMEM((rows, BLOCK), jnp.float32),
                pltpu.VMEM((rows, BLOCK), jnp.float32),
                pltpu.VMEM((rows, HD), jnp.float32),
            ],
        ),
        compiler_params=pltpu.CompilerParams(
            dimension_semantics=("arbitrary",), vmem_limit_bytes=48 * 1024 * 1024
        ),
        cost_estimate=cost,
    )(kidx, cnt, q3, *kv_parts)


def _copy_kernel(x_ref, o_ref):
    o_ref[...] = x_ref[...].reshape(o_ref.shape)


def split_columns(x, parts):
    rows, cols = x.shape
    width = cols // parts
    return pl.pallas_call(
        _copy_kernel,
        out_shape=jax.ShapeDtypeStruct((parts, rows, width), x.dtype),
        grid=(parts,),
        in_specs=[pl.BlockSpec((rows, width), lambda k: (0, k))],
        out_specs=pl.BlockSpec((1, rows, width), lambda k: (k, 0, 0)),
        cost_estimate=pl.CostEstimate(flops=0, transcendentals=0, bytes_accessed=2 * x.size * 2),
    )(x)


def _join_kernel(*refs):
    o_ref = refs[-1]
    rows = refs[0].shape[1]
    for h, x_ref in enumerate(refs[:-1]):
        o_ref[h * rows:(h + 1) * rows, :] = x_ref[0]


def join_columns(parts):
    count, rows, width = parts[0].shape
    total = rows * len(parts)
    return pl.pallas_call(
        _join_kernel,
        out_shape=jax.ShapeDtypeStruct((total, count * width), parts[0].dtype),
        grid=(count,),
        in_specs=[pl.BlockSpec((1, rows, width), lambda k: (k, 0, 0))] * len(parts),
        out_specs=pl.BlockSpec((total, width), lambda k: (0, k)),
        cost_estimate=pl.CostEstimate(
            flops=0, transcendentals=0, bytes_accessed=4 * parts[0].size * len(parts)
        ),
    )(*parts)


def shards(queries, key_states, value_states, page_ids, ref_group, ref_slot):
    n_head = lax.axis_size("head")
    n_ctx = lax.axis_size("ctx")
    tokens = queries.shape[0]
    kv_width = key_states.shape[1]
    kv_heads = kv_width // HD
    q_width = queries.shape[1] // kv_heads
    halves = tokens // BLOCK
    blocks = n_head * halves
    refs = ref_group.shape[1]
    cap = blocks * refs // n_ctx

    kv4 = jnp.stack(
        [
            key_states.reshape(tokens, kv_heads, HD).transpose(1, 0, 2),
            value_states.reshape(tokens, kv_heads, HD).transpose(1, 0, 2),
        ],
        axis=1,
    )
    kv_here = lax.all_to_all(kv4, "head", split_axis=0, concat_axis=0, tiled=True)
    own_kv = (
        kv_here.reshape(n_head, 2, halves, BLOCK, HD).transpose(0, 2, 1, 3, 4).reshape(blocks, 2, BLOCK, HD)
    )

    q_t = split_columns(queries, kv_heads)
    q_here = lax.all_to_all(q_t, "head", split_axis=0, concat_axis=0, tiled=True)

    me = lax.axis_index("ctx")
    rg = ref_group.reshape(n_ctx, blocks * refs)
    rs = ref_slot.reshape(n_ctx, blocks * refs)
    hit = (rg[:, :, None] == jnp.arange(n_ctx, dtype=jnp.int32)[None, None, :]).astype(jnp.int32)
    rank = jnp.sum((jnp.cumsum(hit, axis=1) - 1) * hit, axis=2)
    pick = (rg == me)[:, :, None] & (rank[:, :, None] == jnp.arange(cap, dtype=jnp.int32)[None, None, :])
    send_idx = jnp.sum(jnp.where(pick, rs[:, :, None], 0), axis=1)
    shift = jnp.arange(n_ctx, dtype=jnp.int32)
    send_rolled = jnp.take(send_idx, (me + shift) % n_ctx, axis=0)
    send_kv = jnp.take(own_kv, send_rolled.reshape(-1), axis=0).reshape(n_ctx, cap, 2, BLOCK, HD)
    pieces = []
    for k in range(1, n_ctx):
        route = [(g, g + k) for g in range(n_ctx - k)]
        if k == 1:
            payload = jnp.concatenate([own_kv[blocks - TAIL:], send_kv[1]], axis=0)
            got = lax.ppermute(payload, "ctx", route)
            tail_kv = got[:TAIL]
            pieces.append(got[TAIL:])
        else:
            pieces.append(lax.ppermute(send_kv[k], "ctx", route))
    kv_parts = [tail_kv, own_kv, send_kv[0]] + pieces

    starts = page_starts(page_ids)
    first = me * blocks
    local = jnp.arange(blocks, dtype=jnp.int32)
    gblock = first + local
    st = lax.dynamic_slice_in_dim(starts, first, blocks, 0)
    near_t = jnp.arange(MAXPAGE, dtype=jnp.int32)
    near_ok = (near_t[None, :] == 0) | (near_t[None, :] <= (gblock - st)[:, None])
    near_idx = jnp.where(near_t[None, :] == 0, (local + TAIL)[:, None], (st - first + TAIL - 1)[:, None] + near_t[None, :])
    my_rg = lax.dynamic_slice_in_dim(ref_group, first, blocks, 0)
    my_rs = lax.dynamic_slice_in_dim(ref_slot, first, blocks, 0)
    my_rank = lax.dynamic_index_in_dim(rank, me, 0, keepdims=False).reshape(blocks, refs)
    ref_ok = ((my_rg * blocks + my_rs) < st[:, None]) & (my_rg <= me)
    ref_idx = TAIL + blocks + (me - my_rg) * cap + my_rank
    cand = jnp.concatenate([near_idx, ref_idx], axis=1)
    ok = jnp.concatenate([near_ok, ref_ok], axis=1)
    pos = jnp.cumsum(ok.astype(jnp.int32), axis=1) - 1
    width = MAXPAGE + refs
    slot = jnp.arange(width, dtype=jnp.int32)
    place = ok[:, :, None] & (pos[:, :, None] == slot[None, None, :])
    kidx = jnp.sum(jnp.where(place, cand[:, :, None], 0), axis=1).astype(jnp.int32)
    cnt = jnp.sum(ok.astype(jnp.int32), axis=1).astype(jnp.int32)

    outs = []
    for h in range(halves):
        out_h = attention(kidx, cnt, q_here, kv_parts, h)
        outs.append(lax.all_to_all(out_h, "head", split_axis=0, concat_axis=0, tiled=True))
    return join_columns(outs)


def solution(mesh):
    placed = (
        P(("ctx", "head"), None),
        P(("ctx", "head"), None),
        P(("ctx", "head"), None),
        P(),
        P(),
        P(),
    )
    return jax.shard_map(
        shards, mesh=mesh, in_specs=placed, out_specs=P(("ctx", "head"), None), check_vma=False
    )
```

```python
import functools
import math

import jax
import jax.numpy as jnp
from jax import lax
from jax.experimental import pallas as pl
from jax.experimental.pallas import tpu as pltpu
from jax.sharding import PartitionSpec as P

HD = 128
BLOCK = 128
MAXPAGE = 8
TAIL = MAXPAGE - 1


def page_starts(page_ids):
    block_count = page_ids.shape[0]
    position = jnp.arange(block_count, dtype=jnp.int32)
    is_fresh = jnp.concatenate([jnp.ones((1,), dtype=jnp.bool_), page_ids[1:] != page_ids[:-1]])
    return lax.cummax(jnp.where(is_fresh, position, jnp.zeros_like(position)), axis=0)


def attn_kernel(kidx_ref, cnt_ref, order_ref, q_ref, *rest, scale, group, half, parts):
    kv_parts = rest[:parts]
    o_ref = rest[parts]
    kv_ref, sem, s_scr, m_scr, l_scr, acc_scr = rest[parts + 1:]
    j = pl.program_id(0)

    @pl.when(j == 0)
    def _():
        copies = []
        start = 0
        for idx, part in enumerate(kv_parts):
            size = part.shape[0]
            copy = pltpu.make_async_copy(part, kv_ref.at[pl.ds(start, size)], sem.at[idx])
            copy.start()
            copies.append(copy)
            start += size
        for copy in copies:
            copy.wait()

    b = order_ref[j] * 2 + half
    n = cnt_ref[b]
    diag = TAIL + b
    rows = group * BLOCK
    q_tile = q_ref[0]
    q = jnp.concatenate([q_tile[:, h * HD:(h + 1) * HD] for h in range(group)], axis=0)
    tok = lax.broadcasted_iota(jnp.int32, (rows, BLOCK), 0) % BLOCK
    ahead = lax.broadcasted_iota(jnp.int32, (rows, BLOCK), 1) - tok
    dims = (((1,), (1,)), ((), ()))

    def pair(t, which):
        return jnp.concatenate(
            [kv_ref[kidx_ref[b, t], which], kv_ref[kidx_ref[b, t + 1], which]], axis=0
        )

    s = lax.dot_general(q, kv_ref[diag, 0], dims, preferred_element_type=jnp.float32) * scale
    s = jnp.where(ahead <= 0, s, -1e30)
    s_scr[0] = s
    m_scr[...] = s
    rest = n - 1
    pairs = rest // 2

    def scores(p, carry):
        t = 1 + 2 * p
        s = lax.dot_general(q, pair(t, 0), dims, preferred_element_type=jnp.float32) * scale
        s_scr[t] = s[:, :BLOCK]
        s_scr[t + 1] = s[:, BLOCK:]
        m_scr[...] = jnp.maximum(m_scr[...], jnp.maximum(s[:, :BLOCK], s[:, BLOCK:]))
        return carry

    lax.fori_loop(0, pairs, scores, 0)

    @pl.when(rest % 2 == 1)
    def _():
        t = n - 1
        s = lax.dot_general(q, kv_ref[kidx_ref[b, t], 0], dims, preferred_element_type=jnp.float32) * scale
        s_scr[t] = s
        m_scr[...] = jnp.maximum(m_scr[...], s)

    m = jnp.max(m_scr[...], axis=1, keepdims=True)

    p0 = jnp.exp(s_scr[0] - m)
    l_scr[...] = p0
    acc_scr[...] = jnp.dot(p0.astype(jnp.bfloat16), kv_ref[diag, 1], preferred_element_type=jnp.float32)

    def mix(p, carry):
        t = 1 + 2 * p
        p1 = jnp.exp(s_scr[t] - m)
        p2 = jnp.exp(s_scr[t + 1] - m)
        l_scr[...] += p1 + p2
        w = jnp.concatenate([p1, p2], axis=1).astype(jnp.bfloat16)
        acc_scr[...] += jnp.dot(w, pair(t, 1), preferred_element_type=jnp.float32)
        return carry

    lax.fori_loop(0, pairs, mix, 0)

    @pl.when(rest % 2 == 1)
    def _():
        t = n - 1
        p1 = jnp.exp(s_scr[t] - m)
        l_scr[...] += p1
        acc_scr[...] += jnp.dot(
            p1.astype(jnp.bfloat16), kv_ref[kidx_ref[b, t], 1], preferred_element_type=jnp.float32
        )

    total = jnp.sum(l_scr[...], axis=1, keepdims=True)
    out = acc_scr[...] / total
    for h in range(group):
        o_ref[0, :, h * HD:(h + 1) * HD] = out[h * BLOCK:(h + 1) * BLOCK].astype(o_ref.dtype)


def attention(kidx, cnt, order, q3, kv_parts, half):
    src, width_q = q3.shape[0], q3.shape[2]
    group = width_q // HD
    nk = sum(part.shape[0] for part in kv_parts)
    width = kidx.shape[1]
    rows = group * BLOCK
    q_spec = pl.BlockSpec((1, BLOCK, width_q), lambda j, kidx, cnt, order: (j, half, 0))
    o_spec = pl.BlockSpec((1, BLOCK, width_q), lambda j, kidx, cnt, order: (order[j], 0, 0))
    any_spec = pl.BlockSpec(memory_space=pl.ANY)
    cost = pl.CostEstimate(
        flops=4 * src * 6 * rows * BLOCK * HD,
        transcendentals=src * 6 * rows * BLOCK,
        bytes_accessed=q3.size * 2 + nk * 2 * BLOCK * HD * 2,
    )
    return pl.pallas_call(
        functools.partial(
            attn_kernel, scale=1.0 / math.sqrt(HD), group=group, half=half, parts=len(kv_parts)
        ),
        out_shape=jax.ShapeDtypeStruct((src, BLOCK, width_q), q3.dtype),
        grid_spec=pltpu.PrefetchScalarGridSpec(
            num_scalar_prefetch=3,
            grid=(src,),
            in_specs=[q_spec] + [any_spec] * len(kv_parts),
            out_specs=o_spec,
            scratch_shapes=[
                pltpu.VMEM((nk, 2, BLOCK, HD), jnp.bfloat16),
                pltpu.SemaphoreType.DMA((len(kv_parts),)),
                pltpu.VMEM((width, rows, BLOCK), jnp.float32),
                pltpu.VMEM((rows, BLOCK), jnp.float32),
                pltpu.VMEM((rows, BLOCK), jnp.float32),
                pltpu.VMEM((rows, HD), jnp.float32),
            ],
        ),
        compiler_params=pltpu.CompilerParams(
            dimension_semantics=("arbitrary",), vmem_limit_bytes=48 * 1024 * 1024
        ),
        cost_estimate=cost,
    )(kidx, cnt, order, q3, *kv_parts)


def _copy_kernel(x_ref, o_ref):
    o_ref[...] = x_ref[...].reshape(o_ref.shape)


def split_columns(x, parts):
    rows, cols = x.shape
    width = cols // parts
    return pl.pallas_call(
        _copy_kernel,
        out_shape=jax.ShapeDtypeStruct((parts, rows, width), x.dtype),
        grid=(parts,),
        in_specs=[pl.BlockSpec((rows, width), lambda k: (0, k))],
        out_specs=pl.BlockSpec((1, rows, width), lambda k: (k, 0, 0)),
        cost_estimate=pl.CostEstimate(flops=0, transcendentals=0, bytes_accessed=2 * x.size * 2),
    )(x)


def _join_kernel(*refs):
    o_ref = refs[-1]
    rows = refs[0].shape[1]
    for h, x_ref in enumerate(refs[:-1]):
        o_ref[h * rows:(h + 1) * rows, :] = x_ref[0]


def join_columns(parts):
    count, rows, width = parts[0].shape
    total = rows * len(parts)
    return pl.pallas_call(
        _join_kernel,
        out_shape=jax.ShapeDtypeStruct((total, count * width), parts[0].dtype),
        grid=(count,),
        in_specs=[pl.BlockSpec((1, rows, width), lambda k: (k, 0, 0))] * len(parts),
        out_specs=pl.BlockSpec((total, width), lambda k: (0, k)),
        cost_estimate=pl.CostEstimate(
            flops=0, transcendentals=0, bytes_accessed=4 * parts[0].size * len(parts)
        ),
    )(*parts)


def shards(queries, key_states, value_states, page_ids, ref_group, ref_slot):
    n_head = lax.axis_size("head")
    n_ctx = lax.axis_size("ctx")
    tokens = queries.shape[0]
    kv_width = key_states.shape[1]
    kv_heads = kv_width // HD
    q_width = queries.shape[1] // kv_heads
    halves = tokens // BLOCK
    blocks = n_head * halves
    refs = ref_group.shape[1]
    cap = blocks * refs // n_ctx

    kv4 = jnp.stack(
        [
            key_states.reshape(tokens, kv_heads, HD).transpose(1, 0, 2),
            value_states.reshape(tokens, kv_heads, HD).transpose(1, 0, 2),
        ],
        axis=1,
    )
    kv_here = lax.all_to_all(kv4, "head", split_axis=0, concat_axis=0, tiled=True)
    own_kv = (
        kv_here.reshape(n_head, 2, halves, BLOCK, HD).transpose(0, 2, 1, 3, 4).reshape(blocks, 2, BLOCK, HD)
    )

    me = lax.axis_index("ctx")
    rg = ref_group.reshape(n_ctx, blocks * refs)
    rs = ref_slot.reshape(n_ctx, blocks * refs)
    hit = (rg[:, :, None] == jnp.arange(n_ctx, dtype=jnp.int32)[None, None, :]).astype(jnp.int32)
    rank = jnp.sum((jnp.cumsum(hit, axis=1) - 1) * hit, axis=2)
    pick = (rg == me)[:, :, None] & (rank[:, :, None] == jnp.arange(cap, dtype=jnp.int32)[None, None, :])
    send_idx = jnp.sum(jnp.where(pick, rs[:, :, None], 0), axis=1)
    send_kv = jnp.take(own_kv, send_idx.reshape(-1), axis=0).reshape(n_ctx, cap, 2, BLOCK, HD)
    recv_kv = lax.all_to_all(send_kv, "ctx", split_axis=0, concat_axis=0, tiled=True)

    q_t, _ = lax.optimization_barrier((split_columns(queries, kv_heads), send_kv))
    me_h = lax.axis_index("head")
    q_shift = [lax.dynamic_index_in_dim(q_t, me_h, 0, keepdims=False)]
    for k in range(1, n_head):
        piece = lax.dynamic_index_in_dim(q_t, (me_h + k) % n_head, 0, keepdims=False)
        q_shift.append(lax.ppermute(piece, "head", [(h, (h + k) % n_head) for h in range(n_head)]))
    q_here = jnp.stack(q_shift, axis=0)
    order = ((me_h - jnp.arange(n_head, dtype=jnp.int32)) % n_head).astype(jnp.int32)

    route = [(g, g + 1) for g in range(n_ctx - 1)]
    tail_kv = lax.ppermute(own_kv[blocks - TAIL:], "ctx", route)
    kv_parts = [tail_kv, own_kv, recv_kv.reshape(n_ctx * cap, 2, BLOCK, HD)]

    starts = page_starts(page_ids)
    first = me * blocks
    local = jnp.arange(blocks, dtype=jnp.int32)
    gblock = first + local
    st = lax.dynamic_slice_in_dim(starts, first, blocks, 0)
    near_t = jnp.arange(MAXPAGE, dtype=jnp.int32)
    near_ok = (near_t[None, :] == 0) | (near_t[None, :] <= (gblock - st)[:, None])
    near_idx = jnp.where(near_t[None, :] == 0, (local + TAIL)[:, None], (st - first + TAIL - 1)[:, None] + near_t[None, :])
    my_rg = lax.dynamic_slice_in_dim(ref_group, first, blocks, 0)
    my_rs = lax.dynamic_slice_in_dim(ref_slot, first, blocks, 0)
    my_rank = lax.dynamic_index_in_dim(rank, me, 0, keepdims=False).reshape(blocks, refs)
    ref_ok = (my_rg * blocks + my_rs) < st[:, None]
    ref_idx = TAIL + blocks + my_rg * cap + my_rank
    cand = jnp.concatenate([near_idx, ref_idx], axis=1)
    ok = jnp.concatenate([near_ok, ref_ok], axis=1)
    pos = jnp.cumsum(ok.astype(jnp.int32), axis=1) - 1
    width = MAXPAGE + refs
    slot = jnp.arange(width, dtype=jnp.int32)
    place = ok[:, :, None] & (pos[:, :, None] == slot[None, None, :])
    kidx = jnp.sum(jnp.where(place, cand[:, :, None], 0), axis=1).astype(jnp.int32)
    cnt = jnp.sum(ok.astype(jnp.int32), axis=1).astype(jnp.int32)

    outs = []
    for h in range(halves):
        out_h = attention(kidx, cnt, order, q_here, kv_parts, h)
        outs.append(lax.all_to_all(out_h, "head", split_axis=0, concat_axis=0, tiled=True))
    return join_columns(outs)


def solution(mesh):
    placed = (
        P(("ctx", "head"), None),
        P(("ctx", "head"), None),
        P(("ctx", "head"), None),
        P(),
        P(),
        P(),
    )
    return jax.shard_map(
        shards, mesh=mesh, in_specs=placed, out_specs=P(("ctx", "head"), None), check_vma=False
    )
```

```python
import functools
import math

import jax
import jax.numpy as jnp
from jax import lax
from jax.experimental import pallas as pl
from jax.experimental.pallas import tpu as pltpu
from jax.sharding import PartitionSpec as P

HD = 128
BLOCK = 128
MAXPAGE = 8
TAIL = MAXPAGE - 1


def page_starts(page_ids):
    block_count = page_ids.shape[0]
    position = jnp.arange(block_count, dtype=jnp.int32)
    is_fresh = jnp.concatenate([jnp.ones((1,), dtype=jnp.bool_), page_ids[1:] != page_ids[:-1]])
    return lax.cummax(jnp.where(is_fresh, position, jnp.zeros_like(position)), axis=0)


def attn_kernel(kidx_ref, cnt_ref, order_ref, q_ref, *rest, scale, group, half, parts):
    kv_parts = rest[:parts]
    o_ref = rest[parts]
    kv_ref, sem, s_scr, m_scr, l_scr, acc_scr = rest[parts + 1:]
    j = pl.program_id(0)

    @pl.when(j == 0)
    def _():
        copies = []
        start = 0
        for idx, part in enumerate(kv_parts):
            size = part.shape[0]
            copy = pltpu.make_async_copy(part, kv_ref.at[pl.ds(start, size)], sem.at[idx])
            copy.start()
            copies.append(copy)
            start += size
        for copy in copies:
            copy.wait()

    b = order_ref[j] * 2 + half
    n = cnt_ref[b]
    diag = TAIL + b
    rows = group * BLOCK
    q_tile = q_ref[0]
    q = jnp.concatenate([q_tile[:, h * HD:(h + 1) * HD] for h in range(group)], axis=0)
    tok = lax.broadcasted_iota(jnp.int32, (rows, BLOCK), 0) % BLOCK
    ahead = lax.broadcasted_iota(jnp.int32, (rows, BLOCK), 1) - tok
    dims = (((1,), (1,)), ((), ()))

    def pair(t, which):
        return jnp.concatenate(
            [kv_ref[kidx_ref[b, t], which], kv_ref[kidx_ref[b, t + 1], which]], axis=0
        )

    s = lax.dot_general(q, kv_ref[diag, 0], dims, preferred_element_type=jnp.float32) * scale
    s = jnp.where(ahead <= 0, s, -1e30)
    s_scr[0] = s
    m_scr[...] = s
    rest = n - 1
    pairs = rest // 2

    def scores(p, carry):
        t = 1 + 2 * p
        s = lax.dot_general(q, pair(t, 0), dims, preferred_element_type=jnp.float32) * scale
        s_scr[t] = s[:, :BLOCK]
        s_scr[t + 1] = s[:, BLOCK:]
        m_scr[...] = jnp.maximum(m_scr[...], jnp.maximum(s[:, :BLOCK], s[:, BLOCK:]))
        return carry

    lax.fori_loop(0, pairs, scores, 0)

    @pl.when(rest % 2 == 1)
    def _():
        t = n - 1
        s = lax.dot_general(q, kv_ref[kidx_ref[b, t], 0], dims, preferred_element_type=jnp.float32) * scale
        s_scr[t] = s
        m_scr[...] = jnp.maximum(m_scr[...], s)

    m = jnp.max(m_scr[...], axis=1, keepdims=True)

    p0 = jnp.exp(s_scr[0] - m)
    l_scr[...] = p0
    acc_scr[...] = jnp.dot(p0.astype(jnp.bfloat16), kv_ref[diag, 1], preferred_element_type=jnp.float32)

    def mix(p, carry):
        t = 1 + 2 * p
        p1 = jnp.exp(s_scr[t] - m)
        p2 = jnp.exp(s_scr[t + 1] - m)
        l_scr[...] += p1 + p2
        w = jnp.concatenate([p1, p2], axis=1).astype(jnp.bfloat16)
        acc_scr[...] += jnp.dot(w, pair(t, 1), preferred_element_type=jnp.float32)
        return carry

    lax.fori_loop(0, pairs, mix, 0)

    @pl.when(rest % 2 == 1)
    def _():
        t = n - 1
        p1 = jnp.exp(s_scr[t] - m)
        l_scr[...] += p1
        acc_scr[...] += jnp.dot(
            p1.astype(jnp.bfloat16), kv_ref[kidx_ref[b, t], 1], preferred_element_type=jnp.float32
        )

    total = jnp.sum(l_scr[...], axis=1, keepdims=True)
    out = acc_scr[...] / total
    for h in range(group):
        o_ref[0, :, h * HD:(h + 1) * HD] = out[h * BLOCK:(h + 1) * BLOCK].astype(o_ref.dtype)


def attention(kidx, cnt, order, q3, kv_parts, half, part, split):
    src, width_q = q3.shape[0], q3.shape[2] // split
    group = width_q // HD
    nk = sum(part.shape[0] for part in kv_parts)
    width = kidx.shape[1]
    rows = group * BLOCK
    q_spec = pl.BlockSpec((1, BLOCK, width_q), lambda j, kidx, cnt, order: (j, half, part))
    o_spec = pl.BlockSpec((1, BLOCK, width_q), lambda j, kidx, cnt, order: (order[j], 0, 0))
    any_spec = pl.BlockSpec(memory_space=pl.ANY)
    cost = pl.CostEstimate(
        flops=4 * src * 6 * rows * BLOCK * HD // 2,
        transcendentals=src * 6 * rows * BLOCK,
        bytes_accessed=q3.size * 2 // split + nk * 2 * BLOCK * HD * 2,
    )
    return pl.pallas_call(
        functools.partial(
            attn_kernel, scale=1.0 / math.sqrt(HD), group=group, half=half, parts=len(kv_parts)
        ),
        out_shape=jax.ShapeDtypeStruct((src, BLOCK, width_q), q3.dtype),
        grid_spec=pltpu.PrefetchScalarGridSpec(
            num_scalar_prefetch=3,
            grid=(src,),
            in_specs=[q_spec] + [any_spec] * len(kv_parts),
            out_specs=o_spec,
            scratch_shapes=[
                pltpu.VMEM((nk, 2, BLOCK, HD), jnp.bfloat16),
                pltpu.SemaphoreType.DMA((len(kv_parts),)),
                pltpu.VMEM((width, rows, BLOCK), jnp.float32),
                pltpu.VMEM((rows, BLOCK), jnp.float32),
                pltpu.VMEM((rows, BLOCK), jnp.float32),
                pltpu.VMEM((rows, HD), jnp.float32),
            ],
        ),
        compiler_params=pltpu.CompilerParams(
            dimension_semantics=("arbitrary",), vmem_limit_bytes=48 * 1024 * 1024
        ),
        cost_estimate=cost,
    )(kidx, cnt, order, q3, *kv_parts)


def _copy_kernel(x_ref, o_ref):
    o_ref[...] = x_ref[...].reshape(o_ref.shape)


def split_columns(x, parts):
    rows, cols = x.shape
    width = cols // parts
    return pl.pallas_call(
        _copy_kernel,
        out_shape=jax.ShapeDtypeStruct((parts, rows, width), x.dtype),
        grid=(parts,),
        in_specs=[pl.BlockSpec((rows, width), lambda k: (0, k))],
        out_specs=pl.BlockSpec((1, rows, width), lambda k: (k, 0, 0)),
        cost_estimate=pl.CostEstimate(flops=0, transcendentals=0, bytes_accessed=2 * x.size * 2),
    )(x)


def _join_kernel(*refs):
    o_ref = refs[-1]
    rows, width = refs[0].shape[1], refs[0].shape[2]
    split = o_ref.shape[1] // width
    for idx, x_ref in enumerate(refs[:-1]):
        h, c = divmod(idx, split)
        o_ref[h * rows:(h + 1) * rows, c * width:(c + 1) * width] = x_ref[0]


def join_columns(outs):
    parts = [piece for row in outs for piece in row]
    split = len(outs[0])
    count, rows, width = parts[0].shape
    total = rows * len(outs)
    return pl.pallas_call(
        _join_kernel,
        out_shape=jax.ShapeDtypeStruct((total, count * width * split), parts[0].dtype),
        grid=(count,),
        in_specs=[pl.BlockSpec((1, rows, width), lambda k: (k, 0, 0))] * len(parts),
        out_specs=pl.BlockSpec((total, width * split), lambda k: (0, k)),
        cost_estimate=pl.CostEstimate(
            flops=0, transcendentals=0, bytes_accessed=4 * parts[0].size * len(parts)
        ),
    )(*parts)


def shards(queries, key_states, value_states, page_ids, ref_group, ref_slot):
    n_head = lax.axis_size("head")
    n_ctx = lax.axis_size("ctx")
    tokens = queries.shape[0]
    kv_width = key_states.shape[1]
    kv_heads = kv_width // HD
    q_width = queries.shape[1] // kv_heads
    halves = tokens // BLOCK
    blocks = n_head * halves
    refs = ref_group.shape[1]
    cap = blocks * refs // n_ctx

    kv4 = jnp.stack(
        [
            key_states.reshape(tokens, kv_heads, HD).transpose(1, 0, 2),
            value_states.reshape(tokens, kv_heads, HD).transpose(1, 0, 2),
        ],
        axis=1,
    )
    kv_here = lax.all_to_all(kv4, "head", split_axis=0, concat_axis=0, tiled=True)
    own_kv = (
        kv_here.reshape(n_head, 2, halves, BLOCK, HD).transpose(0, 2, 1, 3, 4).reshape(blocks, 2, BLOCK, HD)
    )

    me = lax.axis_index("ctx")
    rg = ref_group.reshape(n_ctx, blocks * refs)
    rs = ref_slot.reshape(n_ctx, blocks * refs)
    hit = (rg[:, :, None] == jnp.arange(n_ctx, dtype=jnp.int32)[None, None, :]).astype(jnp.int32)
    rank = jnp.sum((jnp.cumsum(hit, axis=1) - 1) * hit, axis=2)
    pick = (rg == me)[:, :, None] & (rank[:, :, None] == jnp.arange(cap, dtype=jnp.int32)[None, None, :])
    send_idx = jnp.sum(jnp.where(pick, rs[:, :, None], 0), axis=1)
    send_kv = jnp.take(own_kv, send_idx.reshape(-1), axis=0).reshape(n_ctx, cap, 2, BLOCK, HD)
    recv_kv = lax.all_to_all(send_kv, "ctx", split_axis=0, concat_axis=0, tiled=True)

    q_t, _ = lax.optimization_barrier((split_columns(queries, kv_heads), send_kv))
    me_h = lax.axis_index("head")
    q_shift = [lax.dynamic_index_in_dim(q_t, me_h, 0, keepdims=False)]
    for k in range(1, n_head):
        piece = lax.dynamic_index_in_dim(q_t, (me_h + k) % n_head, 0, keepdims=False)
        q_shift.append(lax.ppermute(piece, "head", [(h, (h + k) % n_head) for h in range(n_head)]))
    q_here = jnp.stack(q_shift, axis=0)
    order = ((me_h - jnp.arange(n_head, dtype=jnp.int32)) % n_head).astype(jnp.int32)

    route = [(g, g + 1) for g in range(n_ctx - 1)]
    tail_kv = lax.ppermute(own_kv[blocks - TAIL:], "ctx", route)
    kv_parts = [tail_kv, own_kv, recv_kv.reshape(n_ctx * cap, 2, BLOCK, HD)]

    starts = page_starts(page_ids)
    first = me * blocks
    local = jnp.arange(blocks, dtype=jnp.int32)
    gblock = first + local
    st = lax.dynamic_slice_in_dim(starts, first, blocks, 0)
    near_t = jnp.arange(MAXPAGE, dtype=jnp.int32)
    near_ok = (near_t[None, :] == 0) | (near_t[None, :] <= (gblock - st)[:, None])
    near_idx = jnp.where(near_t[None, :] == 0, (local + TAIL)[:, None], (st - first + TAIL - 1)[:, None] + near_t[None, :])
    my_rg = lax.dynamic_slice_in_dim(ref_group, first, blocks, 0)
    my_rs = lax.dynamic_slice_in_dim(ref_slot, first, blocks, 0)
    my_rank = lax.dynamic_index_in_dim(rank, me, 0, keepdims=False).reshape(blocks, refs)
    ref_ok = (my_rg * blocks + my_rs) < st[:, None]
    ref_idx = TAIL + blocks + my_rg * cap + my_rank
    cand = jnp.concatenate([near_idx, ref_idx], axis=1)
    ok = jnp.concatenate([near_ok, ref_ok], axis=1)
    pos = jnp.cumsum(ok.astype(jnp.int32), axis=1) - 1
    width = MAXPAGE + refs
    slot = jnp.arange(width, dtype=jnp.int32)
    place = ok[:, :, None] & (pos[:, :, None] == slot[None, None, :])
    kidx = jnp.sum(jnp.where(place, cand[:, :, None], 0), axis=1).astype(jnp.int32)
    cnt = jnp.sum(ok.astype(jnp.int32), axis=1).astype(jnp.int32)

    split = 2
    outs = []
    for h in range(halves):
        row = []
        for c in range(split):
            out_hc = attention(kidx, cnt, order, q_here, kv_parts, h, c, split)
            row.append(lax.all_to_all(out_hc, "head", split_axis=0, concat_axis=0, tiled=True))
        outs.append(row)
    return join_columns(outs)


def solution(mesh):
    placed = (
        P(("ctx", "head"), None),
        P(("ctx", "head"), None),
        P(("ctx", "head"), None),
        P(),
        P(),
        P(),
    )
    return jax.shard_map(
        shards, mesh=mesh, in_specs=placed, out_specs=P(("ctx", "head"), None), check_vma=False
    )
```

```python
import functools
import math

import jax
import jax.numpy as jnp
from jax import lax
from jax.experimental import pallas as pl
from jax.experimental.pallas import tpu as pltpu
from jax.sharding import PartitionSpec as P

HD = 128
BLOCK = 128
MAXPAGE = 8
TAIL = MAXPAGE - 1


def page_starts(page_ids):
    block_count = page_ids.shape[0]
    position = jnp.arange(block_count, dtype=jnp.int32)
    is_fresh = jnp.concatenate([jnp.ones((1,), dtype=jnp.bool_), page_ids[1:] != page_ids[:-1]])
    return lax.cummax(jnp.where(is_fresh, position, jnp.zeros_like(position)), axis=0)


def attn_kernel(kidx_ref, cnt_ref, order_ref, q_ref, *rest, scale, group, half, parts):
    kv_parts = rest[:parts]
    o_ref = rest[parts]
    kv_ref, sem, s_scr, m_scr, l_scr, acc_scr = rest[parts + 1:]
    j = pl.program_id(0)

    @pl.when(j == 0)
    def _():
        copies = []
        start = 0
        for idx, part in enumerate(kv_parts):
            size = part.shape[0]
            copy = pltpu.make_async_copy(part, kv_ref.at[pl.ds(start, size)], sem.at[idx])
            copy.start()
            copies.append(copy)
            start += size
        for copy in copies:
            copy.wait()

    b = order_ref[j] * 2 + half
    n = cnt_ref[b]
    diag = TAIL + b
    rows = group * BLOCK
    q_tile = q_ref[0]
    q = jnp.concatenate([q_tile[:, h * HD:(h + 1) * HD] for h in range(group)], axis=0)
    tok = lax.broadcasted_iota(jnp.int32, (rows, BLOCK), 0) % BLOCK
    ahead = lax.broadcasted_iota(jnp.int32, (rows, BLOCK), 1) - tok
    dims = (((1,), (1,)), ((), ()))

    def keys(t, size, which):
        return jnp.concatenate([kv_ref[kidx_ref[b, t + i], which] for i in range(size)], axis=0)

    s = lax.dot_general(q, kv_ref[diag, 0], dims, preferred_element_type=jnp.float32) * scale
    s = jnp.where(ahead <= 0, s, -1e30)
    s_scr[0] = s
    m_scr[...] = s
    rest = n - 1
    quads = rest // 4
    tail_start = 1 + 4 * quads
    tail = rest % 4

    def score_step(t, size):
        s = lax.dot_general(q, keys(t, size, 0), dims, preferred_element_type=jnp.float32) * scale
        top = s[:, :BLOCK]
        for i in range(size):
            s_scr[t + i] = s[:, i * BLOCK:(i + 1) * BLOCK]
            if i:
                top = jnp.maximum(top, s[:, i * BLOCK:(i + 1) * BLOCK])
        m_scr[...] = jnp.maximum(m_scr[...], top)

    def scores(p, carry):
        score_step(1 + 4 * p, 4)
        return carry

    lax.fori_loop(0, quads, scores, 0)

    @pl.when(tail >= 2)
    def _():
        score_step(tail_start, 2)

    @pl.when(tail % 2 == 1)
    def _():
        score_step(n - 1, 1)

    m = jnp.max(m_scr[...], axis=1, keepdims=True)

    p0 = jnp.exp(s_scr[0] - m)
    l_scr[...] = p0
    acc_scr[...] = jnp.dot(p0.astype(jnp.bfloat16), kv_ref[diag, 1], preferred_element_type=jnp.float32)

    def mix_step(t, size):
        ps = [jnp.exp(s_scr[t + i] - m) for i in range(size)]
        part = ps[0]
        for p in ps[1:]:
            part = part + p
        l_scr[...] += part
        w = jnp.concatenate(ps, axis=1).astype(jnp.bfloat16) if size > 1 else ps[0].astype(jnp.bfloat16)
        acc_scr[...] += jnp.dot(w, keys(t, size, 1), preferred_element_type=jnp.float32)

    def mix(p, carry):
        mix_step(1 + 4 * p, 4)
        return carry

    lax.fori_loop(0, quads, mix, 0)

    @pl.when(tail >= 2)
    def _():
        mix_step(tail_start, 2)

    @pl.when(tail % 2 == 1)
    def _():
        mix_step(n - 1, 1)

    total = jnp.sum(l_scr[...], axis=1, keepdims=True)
    out = acc_scr[...] / total
    for h in range(group):
        o_ref[0, :, h * HD:(h + 1) * HD] = out[h * BLOCK:(h + 1) * BLOCK].astype(o_ref.dtype)


def attention(kidx, cnt, order, q3, kv_parts, half):
    src, width_q = q3.shape[0], q3.shape[2]
    group = width_q // HD
    nk = sum(part.shape[0] for part in kv_parts)
    width = kidx.shape[1]
    rows = group * BLOCK
    q_spec = pl.BlockSpec((1, BLOCK, width_q), lambda j, kidx, cnt, order: (j, half, 0))
    o_spec = pl.BlockSpec((1, BLOCK, width_q), lambda j, kidx, cnt, order: (order[j], 0, 0))
    any_spec = pl.BlockSpec(memory_space=pl.ANY)
    cost = pl.CostEstimate(
        flops=4 * src * 6 * rows * BLOCK * HD,
        transcendentals=src * 6 * rows * BLOCK,
        bytes_accessed=q3.size * 2 + nk * 2 * BLOCK * HD * 2,
    )
    return pl.pallas_call(
        functools.partial(
            attn_kernel, scale=1.0 / math.sqrt(HD), group=group, half=half, parts=len(kv_parts)
        ),
        out_shape=jax.ShapeDtypeStruct((src, BLOCK, width_q), q3.dtype),
        grid_spec=pltpu.PrefetchScalarGridSpec(
            num_scalar_prefetch=3,
            grid=(src,),
            in_specs=[q_spec] + [any_spec] * len(kv_parts),
            out_specs=o_spec,
            scratch_shapes=[
                pltpu.VMEM((nk, 2, BLOCK, HD), jnp.bfloat16),
                pltpu.SemaphoreType.DMA((len(kv_parts),)),
                pltpu.VMEM((width, rows, BLOCK), jnp.float32),
                pltpu.VMEM((rows, BLOCK), jnp.float32),
                pltpu.VMEM((rows, BLOCK), jnp.float32),
                pltpu.VMEM((rows, HD), jnp.float32),
            ],
        ),
        compiler_params=pltpu.CompilerParams(
            dimension_semantics=("arbitrary",), vmem_limit_bytes=48 * 1024 * 1024
        ),
        cost_estimate=cost,
    )(kidx, cnt, order, q3, *kv_parts)


def _copy_kernel(x_ref, o_ref):
    o_ref[...] = x_ref[...].reshape(o_ref.shape)


def split_columns(x, parts):
    rows, cols = x.shape
    width = cols // parts
    return pl.pallas_call(
        _copy_kernel,
        out_shape=jax.ShapeDtypeStruct((parts, rows, width), x.dtype),
        grid=(parts,),
        in_specs=[pl.BlockSpec((rows, width), lambda k: (0, k))],
        out_specs=pl.BlockSpec((1, rows, width), lambda k: (k, 0, 0)),
        cost_estimate=pl.CostEstimate(flops=0, transcendentals=0, bytes_accessed=2 * x.size * 2),
    )(x)


def _join_kernel(*refs):
    o_ref = refs[-1]
    rows = refs[0].shape[1]
    for h, x_ref in enumerate(refs[:-1]):
        o_ref[h * rows:(h + 1) * rows, :] = x_ref[0]


def join_columns(parts):
    count, rows, width = parts[0].shape
    total = rows * len(parts)
    return pl.pallas_call(
        _join_kernel,
        out_shape=jax.ShapeDtypeStruct((total, count * width), parts[0].dtype),
        grid=(count,),
        in_specs=[pl.BlockSpec((1, rows, width), lambda k: (k, 0, 0))] * len(parts),
        out_specs=pl.BlockSpec((total, width), lambda k: (0, k)),
        cost_estimate=pl.CostEstimate(
            flops=0, transcendentals=0, bytes_accessed=4 * parts[0].size * len(parts)
        ),
    )(*parts)


def shards(queries, key_states, value_states, page_ids, ref_group, ref_slot):
    n_head = lax.axis_size("head")
    n_ctx = lax.axis_size("ctx")
    tokens = queries.shape[0]
    kv_width = key_states.shape[1]
    kv_heads = kv_width // HD
    q_width = queries.shape[1] // kv_heads
    halves = tokens // BLOCK
    blocks = n_head * halves
    refs = ref_group.shape[1]
    cap = blocks * refs // n_ctx

    kv4 = jnp.stack(
        [
            key_states.reshape(tokens, kv_heads, HD).transpose(1, 0, 2),
            value_states.reshape(tokens, kv_heads, HD).transpose(1, 0, 2),
        ],
        axis=1,
    )
    kv_here = lax.all_to_all(kv4, "head", split_axis=0, concat_axis=0, tiled=True)
    own_kv = (
        kv_here.reshape(n_head, 2, halves, BLOCK, HD).transpose(0, 2, 1, 3, 4).reshape(blocks, 2, BLOCK, HD)
    )

    me = lax.axis_index("ctx")
    rg = ref_group.reshape(n_ctx, blocks * refs)
    rs = ref_slot.reshape(n_ctx, blocks * refs)
    hit = (rg[:, :, None] == jnp.arange(n_ctx, dtype=jnp.int32)[None, None, :]).astype(jnp.int32)
    rank = jnp.sum((jnp.cumsum(hit, axis=1) - 1) * hit, axis=2)
    pick = (rg == me)[:, :, None] & (rank[:, :, None] == jnp.arange(cap, dtype=jnp.int32)[None, None, :])
    send_idx = jnp.sum(jnp.where(pick, rs[:, :, None], 0), axis=1)
    send_kv = jnp.take(own_kv, send_idx.reshape(-1), axis=0).reshape(n_ctx, cap, 2, BLOCK, HD)
    recv_kv = lax.all_to_all(send_kv, "ctx", split_axis=0, concat_axis=0, tiled=True)

    q_t, _ = lax.optimization_barrier((split_columns(queries, kv_heads), send_kv))
    me_h = lax.axis_index("head")
    q_shift = [lax.dynamic_index_in_dim(q_t, me_h, 0, keepdims=False)]
    for k in range(1, n_head):
        piece = lax.dynamic_index_in_dim(q_t, (me_h + k) % n_head, 0, keepdims=False)
        q_shift.append(lax.ppermute(piece, "head", [(h, (h + k) % n_head) for h in range(n_head)]))
    q_here = jnp.stack(q_shift, axis=0)
    order = ((me_h - jnp.arange(n_head, dtype=jnp.int32)) % n_head).astype(jnp.int32)

    route = [(g, g + 1) for g in range(n_ctx - 1)]
    tail_kv = lax.ppermute(own_kv[blocks - TAIL:], "ctx", route)
    kv_parts = [tail_kv, own_kv, recv_kv.reshape(n_ctx * cap, 2, BLOCK, HD)]

    starts = page_starts(page_ids)
    first = me * blocks
    local = jnp.arange(blocks, dtype=jnp.int32)
    gblock = first + local
    st = lax.dynamic_slice_in_dim(starts, first, blocks, 0)
    near_t = jnp.arange(MAXPAGE, dtype=jnp.int32)
    near_ok = (near_t[None, :] == 0) | (near_t[None, :] <= (gblock - st)[:, None])
    near_idx = jnp.where(near_t[None, :] == 0, (local + TAIL)[:, None], (st - first + TAIL - 1)[:, None] + near_t[None, :])
    my_rg = lax.dynamic_slice_in_dim(ref_group, first, blocks, 0)
    my_rs = lax.dynamic_slice_in_dim(ref_slot, first, blocks, 0)
    my_rank = lax.dynamic_index_in_dim(rank, me, 0, keepdims=False).reshape(blocks, refs)
    ref_ok = (my_rg * blocks + my_rs) < st[:, None]
    ref_idx = TAIL + blocks + my_rg * cap + my_rank
    cand = jnp.concatenate([near_idx, ref_idx], axis=1)
    ok = jnp.concatenate([near_ok, ref_ok], axis=1)
    pos = jnp.cumsum(ok.astype(jnp.int32), axis=1) - 1
    width = MAXPAGE + refs
    slot = jnp.arange(width, dtype=jnp.int32)
    place = ok[:, :, None] & (pos[:, :, None] == slot[None, None, :])
    kidx = jnp.sum(jnp.where(place, cand[:, :, None], 0), axis=1).astype(jnp.int32)
    cnt = jnp.sum(ok.astype(jnp.int32), axis=1).astype(jnp.int32)

    outs = []
    for h in range(halves):
        out_h = attention(kidx, cnt, order, q_here, kv_parts, h)
        outs.append(lax.all_to_all(out_h, "head", split_axis=0, concat_axis=0, tiled=True))
    return join_columns(outs)


def solution(mesh):
    placed = (
        P(("ctx", "head"), None),
        P(("ctx", "head"), None),
        P(("ctx", "head"), None),
        P(),
        P(),
        P(),
    )
    return jax.shard_map(
        shards, mesh=mesh, in_specs=placed, out_specs=P(("ctx", "head"), None), check_vma=False
    )
```

```python
import functools
import math

import jax
import jax.numpy as jnp
from jax import lax
from jax.experimental import pallas as pl
from jax.experimental.pallas import tpu as pltpu
from jax.sharding import PartitionSpec as P

HD = 128
BLOCK = 128
MAXPAGE = 8
TAIL = MAXPAGE - 1


def page_starts(page_ids):
    block_count = page_ids.shape[0]
    position = jnp.arange(block_count, dtype=jnp.int32)
    is_fresh = jnp.concatenate([jnp.ones((1,), dtype=jnp.bool_), page_ids[1:] != page_ids[:-1]])
    return lax.cummax(jnp.where(is_fresh, position, jnp.zeros_like(position)), axis=0)


def attn_kernel(kidx_ref, cnt_ref, order_ref, q_ref, *rest, scale, group, half, parts):
    kv_parts = rest[:parts]
    o_ref = rest[parts]
    kv_ref, sem, s_scr, m_scr, l_scr, acc_scr = rest[parts + 1:]
    j = pl.program_id(0)

    @pl.when(j == 0)
    def _():
        copies = []
        start = 0
        for idx, part in enumerate(kv_parts):
            size = part.shape[0]
            copy = pltpu.make_async_copy(part, kv_ref.at[pl.ds(start, size)], sem.at[idx])
            copy.start()
            copies.append(copy)
            start += size
        for copy in copies:
            copy.wait()

    b = order_ref[j] * 2 + half
    n = cnt_ref[b]
    diag = TAIL + b
    rows = group * BLOCK
    q_tile = q_ref[0]
    q = jnp.concatenate([q_tile[:, h * HD:(h + 1) * HD] for h in range(group)], axis=0)
    tok = lax.broadcasted_iota(jnp.int32, (rows, BLOCK), 0) % BLOCK
    ahead = lax.broadcasted_iota(jnp.int32, (rows, BLOCK), 1) - tok
    dims = (((1,), (1,)), ((), ()))

    def pair(t, which):
        return jnp.concatenate(
            [kv_ref[kidx_ref[b, t], which], kv_ref[kidx_ref[b, t + 1], which]], axis=0
        )

    s = lax.dot_general(q, kv_ref[diag, 0], dims, preferred_element_type=jnp.float32) * scale
    s = jnp.where(ahead <= 0, s, -1e30)
    s_scr[0] = s
    m_scr[...] = s
    rest = n - 1
    pairs = rest // 2

    def scores(p, carry):
        t = 1 + 2 * p
        s = lax.dot_general(q, pair(t, 0), dims, preferred_element_type=jnp.float32) * scale
        s_scr[t] = s[:, :BLOCK]
        s_scr[t + 1] = s[:, BLOCK:]
        m_scr[...] = jnp.maximum(m_scr[...], jnp.maximum(s[:, :BLOCK], s[:, BLOCK:]))
        return carry

    lax.fori_loop(0, pairs, scores, 0)

    @pl.when(rest % 2 == 1)
    def _():
        t = n - 1
        s = lax.dot_general(q, kv_ref[kidx_ref[b, t], 0], dims, preferred_element_type=jnp.float32) * scale
        s_scr[t] = s
        m_scr[...] = jnp.maximum(m_scr[...], s)

    m = jnp.max(m_scr[...], axis=1, keepdims=True)

    p0 = jnp.exp(s_scr[0] - m)
    l_scr[...] = p0
    acc_scr[...] = jnp.dot(p0.astype(jnp.bfloat16), kv_ref[diag, 1], preferred_element_type=jnp.float32)

    def mix(p, carry):
        t = 1 + 2 * p
        p1 = jnp.exp(s_scr[t] - m)
        p2 = jnp.exp(s_scr[t + 1] - m)
        l_scr[...] += p1 + p2
        w = jnp.concatenate([p1, p2], axis=1).astype(jnp.bfloat16)
        acc_scr[...] += jnp.dot(w, pair(t, 1), preferred_element_type=jnp.float32)
        return carry

    lax.fori_loop(0, pairs, mix, 0)

    @pl.when(rest % 2 == 1)
    def _():
        t = n - 1
        p1 = jnp.exp(s_scr[t] - m)
        l_scr[...] += p1
        acc_scr[...] += jnp.dot(
            p1.astype(jnp.bfloat16), kv_ref[kidx_ref[b, t], 1], preferred_element_type=jnp.float32
        )

    total = jnp.sum(l_scr[...], axis=1, keepdims=True)
    out = acc_scr[...] / total
    for h in range(group):
        o_ref[0, :, h * HD:(h + 1) * HD] = out[h * BLOCK:(h + 1) * BLOCK].astype(o_ref.dtype)


def attention(kidx, cnt, order, q3, kv_parts, half):
    src, width_q = q3.shape[0], q3.shape[2]
    group = width_q // HD
    nk = sum(part.shape[0] for part in kv_parts)
    width = kidx.shape[1]
    rows = group * BLOCK
    q_spec = pl.BlockSpec((1, BLOCK, width_q), lambda j, kidx, cnt, order: (j, half, 0))
    o_spec = pl.BlockSpec((1, BLOCK, width_q), lambda j, kidx, cnt, order: (order[j], 0, 0))
    any_spec = pl.BlockSpec(memory_space=pl.ANY)
    cost = pl.CostEstimate(
        flops=4 * src * 6 * rows * BLOCK * HD,
        transcendentals=src * 6 * rows * BLOCK,
        bytes_accessed=q3.size * 2 + nk * 2 * BLOCK * HD * 2,
    )
    return pl.pallas_call(
        functools.partial(
            attn_kernel, scale=1.0 / math.sqrt(HD), group=group, half=half, parts=len(kv_parts)
        ),
        out_shape=jax.ShapeDtypeStruct((src, BLOCK, width_q), q3.dtype),
        grid_spec=pltpu.PrefetchScalarGridSpec(
            num_scalar_prefetch=3,
            grid=(src,),
            in_specs=[q_spec] + [any_spec] * len(kv_parts),
            out_specs=o_spec,
            scratch_shapes=[
                pltpu.VMEM((nk, 2, BLOCK, HD), jnp.bfloat16),
                pltpu.SemaphoreType.DMA((len(kv_parts),)),
                pltpu.VMEM((width, rows, BLOCK), jnp.float32),
                pltpu.VMEM((rows, BLOCK), jnp.float32),
                pltpu.VMEM((rows, BLOCK), jnp.float32),
                pltpu.VMEM((rows, HD), jnp.float32),
            ],
        ),
        compiler_params=pltpu.CompilerParams(
            dimension_semantics=("arbitrary",), vmem_limit_bytes=48 * 1024 * 1024
        ),
        cost_estimate=cost,
    )(kidx, cnt, order, q3, *kv_parts)


def _copy_kernel(x_ref, o_ref):
    o_ref[...] = x_ref[...].reshape(o_ref.shape)


def split_columns(x, parts):
    rows, cols = x.shape
    width = cols // parts
    return pl.pallas_call(
        _copy_kernel,
        out_shape=jax.ShapeDtypeStruct((parts, rows, width), x.dtype),
        grid=(parts,),
        in_specs=[pl.BlockSpec((rows, width), lambda k: (0, k))],
        out_specs=pl.BlockSpec((1, rows, width), lambda k: (k, 0, 0)),
        cost_estimate=pl.CostEstimate(flops=0, transcendentals=0, bytes_accessed=2 * x.size * 2),
    )(x)


def _join_kernel(*refs):
    o_ref = refs[-1]
    rows = refs[0].shape[1]
    for h, x_ref in enumerate(refs[:-1]):
        o_ref[h * rows:(h + 1) * rows, :] = x_ref[0]


def join_columns(parts):
    count, rows, width = parts[0].shape
    total = rows * len(parts)
    return pl.pallas_call(
        _join_kernel,
        out_shape=jax.ShapeDtypeStruct((total, count * width), parts[0].dtype),
        grid=(count,),
        in_specs=[pl.BlockSpec((1, rows, width), lambda k: (k, 0, 0))] * len(parts),
        out_specs=pl.BlockSpec((total, width), lambda k: (0, k)),
        cost_estimate=pl.CostEstimate(
            flops=0, transcendentals=0, bytes_accessed=4 * parts[0].size * len(parts)
        ),
    )(*parts)


def shards(queries, key_states, value_states, page_ids, ref_group, ref_slot):
    n_head = lax.axis_size("head")
    n_ctx = lax.axis_size("ctx")
    tokens = queries.shape[0]
    kv_width = key_states.shape[1]
    kv_heads = kv_width // HD
    q_width = queries.shape[1] // kv_heads
    halves = tokens // BLOCK
    blocks = n_head * halves
    refs = ref_group.shape[1]
    cap = blocks * refs // n_ctx

    kv4 = jnp.stack(
        [
            key_states.reshape(tokens, kv_heads, HD).transpose(1, 0, 2),
            value_states.reshape(tokens, kv_heads, HD).transpose(1, 0, 2),
        ],
        axis=1,
    )
    kv_here = lax.all_to_all(kv4, "head", split_axis=0, concat_axis=0, tiled=True)
    own_kv = (
        kv_here.reshape(n_head, 2, halves, BLOCK, HD).transpose(0, 2, 1, 3, 4).reshape(blocks, 2, BLOCK, HD)
    )

    me = lax.axis_index("ctx")
    rg = ref_group.reshape(n_ctx, blocks * refs)
    rs = ref_slot.reshape(n_ctx, blocks * refs)
    hit = (rg[:, :, None] == jnp.arange(n_ctx, dtype=jnp.int32)[None, None, :]).astype(jnp.int32)
    rank = jnp.sum((jnp.cumsum(hit, axis=1) - 1) * hit, axis=2)
    pick = (rg == me)[:, :, None] & (rank[:, :, None] == jnp.arange(cap, dtype=jnp.int32)[None, None, :])
    send_idx = jnp.sum(jnp.where(pick, rs[:, :, None], 0), axis=1)
    send_kv = jnp.take(own_kv, send_idx.reshape(-1), axis=0, mode="clip").reshape(n_ctx, cap, 2, BLOCK, HD)
    recv_kv = lax.all_to_all(send_kv, "ctx", split_axis=0, concat_axis=0, tiled=True)

    q_t, _ = lax.optimization_barrier((split_columns(queries, kv_heads), send_kv))
    me_h = lax.axis_index("head")
    q_shift = [lax.dynamic_index_in_dim(q_t, me_h, 0, keepdims=False)]
    for k in range(1, n_head):
        piece = lax.dynamic_index_in_dim(q_t, (me_h + k) % n_head, 0, keepdims=False)
        q_shift.append(lax.ppermute(piece, "head", [(h, (h + k) % n_head) for h in range(n_head)]))
    q_here = jnp.stack(q_shift, axis=0)
    order = ((me_h - jnp.arange(n_head, dtype=jnp.int32)) % n_head).astype(jnp.int32)

    route = [(g, g + 1) for g in range(n_ctx - 1)]
    tail_kv = lax.ppermute(own_kv[blocks - TAIL:], "ctx", route)
    kv_parts = [tail_kv, own_kv, recv_kv.reshape(n_ctx * cap, 2, BLOCK, HD)]

    starts = page_starts(page_ids)
    first = me * blocks
    local = jnp.arange(blocks, dtype=jnp.int32)
    gblock = first + local
    st = lax.dynamic_slice_in_dim(starts, first, blocks, 0)
    near_t = jnp.arange(MAXPAGE, dtype=jnp.int32)
    near_ok = (near_t[None, :] == 0) | (near_t[None, :] <= (gblock - st)[:, None])
    near_idx = jnp.where(near_t[None, :] == 0, (local + TAIL)[:, None], (st - first + TAIL - 1)[:, None] + near_t[None, :])
    my_rg = lax.dynamic_slice_in_dim(ref_group, first, blocks, 0)
    my_rs = lax.dynamic_slice_in_dim(ref_slot, first, blocks, 0)
    my_rank = lax.dynamic_index_in_dim(rank, me, 0, keepdims=False).reshape(blocks, refs)
    ref_ok = (my_rg * blocks + my_rs) < st[:, None]
    ref_idx = TAIL + blocks + my_rg * cap + my_rank
    cand = jnp.concatenate([near_idx, ref_idx], axis=1)
    ok = jnp.concatenate([near_ok, ref_ok], axis=1)
    pos = jnp.cumsum(ok.astype(jnp.int32), axis=1) - 1
    width = MAXPAGE + refs
    slot = jnp.arange(width, dtype=jnp.int32)
    place = ok[:, :, None] & (pos[:, :, None] == slot[None, None, :])
    kidx = jnp.sum(jnp.where(place, cand[:, :, None], 0), axis=1).astype(jnp.int32)
    cnt = jnp.sum(ok.astype(jnp.int32), axis=1).astype(jnp.int32)

    outs = []
    for h in range(halves):
        out_h = attention(kidx, cnt, order, q_here, kv_parts, h)
        outs.append(lax.all_to_all(out_h, "head", split_axis=0, concat_axis=0, tiled=True))
    return join_columns(outs)


def solution(mesh):
    placed = (
        P(("ctx", "head"), None),
        P(("ctx", "head"), None),
        P(("ctx", "head"), None),
        P(),
        P(),
        P(),
    )
    return jax.shard_map(
        shards, mesh=mesh, in_specs=placed, out_specs=P(("ctx", "head"), None), check_vma=False
    )
```

```python
import functools
import math

import jax
import jax.numpy as jnp
from jax import lax
from jax.experimental import pallas as pl
from jax.experimental.pallas import tpu as pltpu
from jax.sharding import PartitionSpec as P

HD = 128
BLOCK = 128
MAXPAGE = 8
TAIL = MAXPAGE - 1


def page_starts(page_ids):
    block_count = page_ids.shape[0]
    position = jnp.arange(block_count, dtype=jnp.int32)
    is_fresh = jnp.concatenate([jnp.ones((1,), dtype=jnp.bool_), page_ids[1:] != page_ids[:-1]])
    return lax.cummax(jnp.where(is_fresh, position, jnp.zeros_like(position)), axis=0)


def attn_kernel(kidx_ref, cnt_ref, order_ref, q_ref, *rest, scale, group, half, parts):
    kv_parts = rest[:parts]
    o_ref = rest[parts]
    kv_ref, sem, s_scr, m_scr, l_scr, acc_scr = rest[parts + 1:]
    j = pl.program_id(0)

    @pl.when(j == 0)
    def _():
        copies = []
        start = 0
        for idx, part in enumerate(kv_parts):
            size = part.shape[0]
            copy = pltpu.make_async_copy(part, kv_ref.at[pl.ds(start, size)], sem.at[idx])
            copy.start()
            copies.append(copy)
            start += size
        for copy in copies:
            copy.wait()

    b = order_ref[j] * 2 + half
    n = cnt_ref[b]
    diag = TAIL + b
    rows = group * BLOCK
    q_tile = q_ref[0]
    q = jnp.concatenate([q_tile[:, h * HD:(h + 1) * HD] for h in range(group)], axis=0)
    tok = lax.broadcasted_iota(jnp.int32, (rows, BLOCK), 0) % BLOCK
    ahead = lax.broadcasted_iota(jnp.int32, (rows, BLOCK), 1) - tok
    dims = (((1,), (1,)), ((), ()))

    def pair(t, which):
        return jnp.concatenate(
            [kv_ref[kidx_ref[b, t], which], kv_ref[kidx_ref[b, t + 1], which]], axis=0
        )

    s = lax.dot_general(q, kv_ref[diag, 0], dims, preferred_element_type=jnp.float32) * scale
    s = jnp.where(ahead <= 0, s, -1e30)
    s_scr[0] = s
    m_scr[...] = s
    rest = n - 1
    pairs = rest // 2

    def scores(p, carry):
        t = 1 + 2 * p
        s = lax.dot_general(q, pair(t, 0), dims, preferred_element_type=jnp.float32) * scale
        s_scr[t] = s[:, :BLOCK]
        s_scr[t + 1] = s[:, BLOCK:]
        m_scr[...] = jnp.maximum(m_scr[...], jnp.maximum(s[:, :BLOCK], s[:, BLOCK:]))
        return carry

    lax.fori_loop(0, pairs, scores, 0)

    @pl.when(rest % 2 == 1)
    def _():
        t = n - 1
        s = lax.dot_general(q, kv_ref[kidx_ref[b, t], 0], dims, preferred_element_type=jnp.float32) * scale
        s_scr[t] = s
        m_scr[...] = jnp.maximum(m_scr[...], s)

    m = jnp.max(m_scr[...], axis=1, keepdims=True)

    p0 = jnp.exp(s_scr[0] - m)
    l_scr[...] = p0
    acc_scr[...] = jnp.dot(p0.astype(jnp.bfloat16), kv_ref[diag, 1], preferred_element_type=jnp.float32)

    def mix(p, carry):
        t = 1 + 2 * p
        p1 = jnp.exp(s_scr[t] - m)
        p2 = jnp.exp(s_scr[t + 1] - m)
        l_scr[...] += p1 + p2
        w = jnp.concatenate([p1, p2], axis=1).astype(jnp.bfloat16)
        acc_scr[...] += jnp.dot(w, pair(t, 1), preferred_element_type=jnp.float32)
        return carry

    lax.fori_loop(0, pairs, mix, 0)

    @pl.when(rest % 2 == 1)
    def _():
        t = n - 1
        p1 = jnp.exp(s_scr[t] - m)
        l_scr[...] += p1
        acc_scr[...] += jnp.dot(
            p1.astype(jnp.bfloat16), kv_ref[kidx_ref[b, t], 1], preferred_element_type=jnp.float32
        )

    total = jnp.sum(l_scr[...], axis=1, keepdims=True)
    out = acc_scr[...] / total
    for h in range(group):
        o_ref[0, :, h * HD:(h + 1) * HD] = out[h * BLOCK:(h + 1) * BLOCK].astype(o_ref.dtype)


def attention(kidx, cnt, order, q3, kv_parts, half):
    src, width_q = q3.shape[0], q3.shape[2]
    group = width_q // HD
    nk = sum(part.shape[0] for part in kv_parts)
    width = kidx.shape[1]
    rows = group * BLOCK
    q_spec = pl.BlockSpec((1, BLOCK, width_q), lambda j, kidx, cnt, order: (j, half, 0))
    o_spec = pl.BlockSpec((1, BLOCK, width_q), lambda j, kidx, cnt, order: (order[j], 0, 0))
    any_spec = pl.BlockSpec(memory_space=pl.ANY)
    cost = pl.CostEstimate(
        flops=4 * src * 6 * rows * BLOCK * HD,
        transcendentals=src * 6 * rows * BLOCK,
        bytes_accessed=q3.size * 2 + nk * 2 * BLOCK * HD * 2,
    )
    return pl.pallas_call(
        functools.partial(
            attn_kernel, scale=1.0 / math.sqrt(HD), group=group, half=half, parts=len(kv_parts)
        ),
        out_shape=jax.ShapeDtypeStruct((src, BLOCK, width_q), q3.dtype),
        grid_spec=pltpu.PrefetchScalarGridSpec(
            num_scalar_prefetch=3,
            grid=(src,),
            in_specs=[q_spec] + [any_spec] * len(kv_parts),
            out_specs=o_spec,
            scratch_shapes=[
                pltpu.VMEM((nk, 2, BLOCK, HD), jnp.bfloat16),
                pltpu.SemaphoreType.DMA((len(kv_parts),)),
                pltpu.VMEM((width, rows, BLOCK), jnp.float32),
                pltpu.VMEM((rows, BLOCK), jnp.float32),
                pltpu.VMEM((rows, BLOCK), jnp.float32),
                pltpu.VMEM((rows, HD), jnp.float32),
            ],
        ),
        compiler_params=pltpu.CompilerParams(
            dimension_semantics=("arbitrary",), vmem_limit_bytes=48 * 1024 * 1024
        ),
        cost_estimate=cost,
    )(kidx, cnt, order, q3, *kv_parts)


def _copy_kernel(x_ref, o_ref):
    o_ref[...] = x_ref[...].reshape(o_ref.shape)


def _rot_copy_kernel(rot_ref, x_ref, o_ref):
    o_ref[...] = x_ref[...].reshape(o_ref.shape)


def split_columns(x, parts, rot):
    rows, cols = x.shape
    width = cols // parts
    return pl.pallas_call(
        _rot_copy_kernel,
        out_shape=jax.ShapeDtypeStruct((parts, rows, width), x.dtype),
        grid_spec=pltpu.PrefetchScalarGridSpec(
            num_scalar_prefetch=1,
            grid=(parts,),
            in_specs=[pl.BlockSpec((rows, width), lambda k, rot: (0, (k + rot[0]) % parts))],
            out_specs=pl.BlockSpec((1, rows, width), lambda k, rot: (k, 0, 0)),
        ),
        cost_estimate=pl.CostEstimate(flops=0, transcendentals=0, bytes_accessed=2 * x.size * 2),
    )(rot, x)


def _join_kernel(*refs):
    o_ref = refs[-1]
    rows = refs[0].shape[1]
    for h, x_ref in enumerate(refs[:-1]):
        o_ref[h * rows:(h + 1) * rows, :] = x_ref[0]


def join_columns(parts):
    count, rows, width = parts[0].shape
    total = rows * len(parts)
    return pl.pallas_call(
        _join_kernel,
        out_shape=jax.ShapeDtypeStruct((total, count * width), parts[0].dtype),
        grid=(count,),
        in_specs=[pl.BlockSpec((1, rows, width), lambda k: (k, 0, 0))] * len(parts),
        out_specs=pl.BlockSpec((total, width), lambda k: (0, k)),
        cost_estimate=pl.CostEstimate(
            flops=0, transcendentals=0, bytes_accessed=4 * parts[0].size * len(parts)
        ),
    )(*parts)


def shards(queries, key_states, value_states, page_ids, ref_group, ref_slot):
    n_head = lax.axis_size("head")
    n_ctx = lax.axis_size("ctx")
    tokens = queries.shape[0]
    kv_width = key_states.shape[1]
    kv_heads = kv_width // HD
    q_width = queries.shape[1] // kv_heads
    halves = tokens // BLOCK
    blocks = n_head * halves
    refs = ref_group.shape[1]
    cap = blocks * refs // n_ctx

    kv4 = jnp.stack(
        [
            key_states.reshape(tokens, kv_heads, HD).transpose(1, 0, 2),
            value_states.reshape(tokens, kv_heads, HD).transpose(1, 0, 2),
        ],
        axis=1,
    )
    kv_here = lax.all_to_all(kv4, "head", split_axis=0, concat_axis=0, tiled=True)
    own_kv = (
        kv_here.reshape(n_head, 2, halves, BLOCK, HD).transpose(0, 2, 1, 3, 4).reshape(blocks, 2, BLOCK, HD)
    )

    me = lax.axis_index("ctx")
    rg = ref_group.reshape(n_ctx, blocks * refs)
    rs = ref_slot.reshape(n_ctx, blocks * refs)
    hit = (rg[:, :, None] == jnp.arange(n_ctx, dtype=jnp.int32)[None, None, :]).astype(jnp.int32)
    rank = jnp.sum((jnp.cumsum(hit, axis=1) - 1) * hit, axis=2)
    pick = (rg == me)[:, :, None] & (rank[:, :, None] == jnp.arange(cap, dtype=jnp.int32)[None, None, :])
    send_idx = jnp.sum(jnp.where(pick, rs[:, :, None], 0), axis=1)
    send_kv = jnp.take(own_kv, send_idx.reshape(-1), axis=0, mode="clip").reshape(n_ctx, cap, 2, BLOCK, HD)
    recv_kv = lax.all_to_all(send_kv, "ctx", split_axis=0, concat_axis=0, tiled=True)

    me_h = lax.axis_index("head")
    rot = jnp.reshape(me_h, (1,)).astype(jnp.int32)
    q_t, _ = lax.optimization_barrier((split_columns(queries, kv_heads, rot), send_kv))
    q_shift = [q_t[0]]
    for k in range(1, n_head):
        q_shift.append(lax.ppermute(q_t[k], "head", [(h, (h + k) % n_head) for h in range(n_head)]))
    q_here = jnp.stack(q_shift, axis=0)
    order = ((me_h - jnp.arange(n_head, dtype=jnp.int32)) % n_head).astype(jnp.int32)

    route = [(g, g + 1) for g in range(n_ctx - 1)]
    tail_kv = lax.ppermute(own_kv[blocks - TAIL:], "ctx", route)
    kv_parts = [tail_kv, own_kv, recv_kv.reshape(n_ctx * cap, 2, BLOCK, HD)]

    starts = page_starts(page_ids)
    first = me * blocks
    local = jnp.arange(blocks, dtype=jnp.int32)
    gblock = first + local
    st = lax.dynamic_slice_in_dim(starts, first, blocks, 0)
    near_t = jnp.arange(MAXPAGE, dtype=jnp.int32)
    near_ok = (near_t[None, :] == 0) | (near_t[None, :] <= (gblock - st)[:, None])
    near_idx = jnp.where(near_t[None, :] == 0, (local + TAIL)[:, None], (st - first + TAIL - 1)[:, None] + near_t[None, :])
    my_rg = lax.dynamic_slice_in_dim(ref_group, first, blocks, 0)
    my_rs = lax.dynamic_slice_in_dim(ref_slot, first, blocks, 0)
    my_rank = lax.dynamic_index_in_dim(rank, me, 0, keepdims=False).reshape(blocks, refs)
    ref_ok = (my_rg * blocks + my_rs) < st[:, None]
    ref_idx = TAIL + blocks + my_rg * cap + my_rank
    cand = jnp.concatenate([near_idx, ref_idx], axis=1)
    ok = jnp.concatenate([near_ok, ref_ok], axis=1)
    pos = jnp.cumsum(ok.astype(jnp.int32), axis=1) - 1
    width = MAXPAGE + refs
    slot = jnp.arange(width, dtype=jnp.int32)
    place = ok[:, :, None] & (pos[:, :, None] == slot[None, None, :])
    kidx = jnp.sum(jnp.where(place, cand[:, :, None], 0), axis=1).astype(jnp.int32)
    cnt = jnp.sum(ok.astype(jnp.int32), axis=1).astype(jnp.int32)

    outs = []
    for h in range(halves):
        out_h = attention(kidx, cnt, order, q_here, kv_parts, h)
        outs.append(lax.all_to_all(out_h, "head", split_axis=0, concat_axis=0, tiled=True))
    return join_columns(outs)


def solution(mesh):
    placed = (
        P(("ctx", "head"), None),
        P(("ctx", "head"), None),
        P(("ctx", "head"), None),
        P(),
        P(),
        P(),
    )
    return jax.shard_map(
        shards, mesh=mesh, in_specs=placed, out_specs=P(("ctx", "head"), None), check_vma=False
    )
```

```python
import functools
import math

import jax
import jax.numpy as jnp
from jax import lax
from jax.experimental import pallas as pl
from jax.experimental.pallas import tpu as pltpu
from jax.sharding import PartitionSpec as P

HD = 128
BLOCK = 128
MAXPAGE = 8
TAIL = MAXPAGE - 1


def page_starts(page_ids):
    block_count = page_ids.shape[0]
    position = jnp.arange(block_count, dtype=jnp.int32)
    is_fresh = jnp.concatenate([jnp.ones((1,), dtype=jnp.bool_), page_ids[1:] != page_ids[:-1]])
    return lax.cummax(jnp.where(is_fresh, position, jnp.zeros_like(position)), axis=0)


def attn_kernel(kidx_ref, cnt_ref, order_ref, q_ref, *rest, scale, group, half, parts):
    kv_parts = rest[:parts]
    o_ref = rest[parts]
    kv_ref, sem, s_scr, m_scr, l_scr, acc_scr = rest[parts + 1:]
    j = pl.program_id(0)

    @pl.when(j == 0)
    def _():
        copies = []
        start = 0
        for idx, part in enumerate(kv_parts):
            size = part.shape[0]
            copy = pltpu.make_async_copy(part, kv_ref.at[pl.ds(start, size)], sem.at[idx])
            copy.start()
            copies.append(copy)
            start += size
        for copy in copies:
            copy.wait()

    b = order_ref[j] * 2 + half
    n = cnt_ref[b]
    diag = TAIL + b
    rows = group * BLOCK
    q_tile = q_ref[0]
    q = jnp.concatenate([q_tile[:, h * HD:(h + 1) * HD] for h in range(group)], axis=0)
    tok = lax.broadcasted_iota(jnp.int32, (rows, BLOCK), 0) % BLOCK
    ahead = lax.broadcasted_iota(jnp.int32, (rows, BLOCK), 1) - tok
    dims = (((1,), (1,)), ((), ()))

    def pair(t, which):
        return jnp.concatenate(
            [kv_ref[kidx_ref[b, t], which], kv_ref[kidx_ref[b, t + 1], which]], axis=0
        )

    s = lax.dot_general(q, kv_ref[diag, 0], dims, preferred_element_type=jnp.float32) * scale
    s = jnp.where(ahead <= 0, s, -1e30)
    s_scr[0] = s
    m_scr[...] = s
    rest = n - 1
    pairs = rest // 2

    def scores(p, carry):
        t = 1 + 2 * p
        s = lax.dot_general(q, pair(t, 0), dims, preferred_element_type=jnp.float32) * scale
        s_scr[t] = s[:, :BLOCK]
        s_scr[t + 1] = s[:, BLOCK:]
        m_scr[...] = jnp.maximum(m_scr[...], jnp.maximum(s[:, :BLOCK], s[:, BLOCK:]))
        return carry

    lax.fori_loop(0, pairs, scores, 0)

    @pl.when(rest % 2 == 1)
    def _():
        t = n - 1
        s = lax.dot_general(q, kv_ref[kidx_ref[b, t], 0], dims, preferred_element_type=jnp.float32) * scale
        s_scr[t] = s
        m_scr[...] = jnp.maximum(m_scr[...], s)

    m = jnp.max(m_scr[...], axis=1, keepdims=True)

    p0 = jnp.exp(s_scr[0] - m)
    l_scr[...] = p0
    acc_scr[...] = jnp.dot(p0.astype(jnp.bfloat16), kv_ref[diag, 1], preferred_element_type=jnp.float32)

    def mix(p, carry):
        t = 1 + 2 * p
        p1 = jnp.exp(s_scr[t] - m)
        p2 = jnp.exp(s_scr[t + 1] - m)
        l_scr[...] += p1 + p2
        w = jnp.concatenate([p1, p2], axis=1).astype(jnp.bfloat16)
        acc_scr[...] += jnp.dot(w, pair(t, 1), preferred_element_type=jnp.float32)
        return carry

    lax.fori_loop(0, pairs, mix, 0)

    @pl.when(rest % 2 == 1)
    def _():
        t = n - 1
        p1 = jnp.exp(s_scr[t] - m)
        l_scr[...] += p1
        acc_scr[...] += jnp.dot(
            p1.astype(jnp.bfloat16), kv_ref[kidx_ref[b, t], 1], preferred_element_type=jnp.float32
        )

    total = jnp.sum(l_scr[...], axis=1, keepdims=True)
    out = acc_scr[...] / total
    for h in range(group):
        o_ref[0, :, h * HD:(h + 1) * HD] = out[h * BLOCK:(h + 1) * BLOCK].astype(o_ref.dtype)


def attention(kidx, cnt, order, q3, kv_parts, half):
    src, width_q = q3.shape[0], q3.shape[2]
    group = width_q // HD
    nk = sum(part.shape[0] for part in kv_parts)
    width = kidx.shape[1]
    rows = group * BLOCK
    q_spec = pl.BlockSpec((1, BLOCK, width_q), lambda j, kidx, cnt, order: (j, half, 0))
    o_spec = pl.BlockSpec((1, BLOCK, width_q), lambda j, kidx, cnt, order: (order[j], 0, 0))
    any_spec = pl.BlockSpec(memory_space=pl.ANY)
    cost = pl.CostEstimate(
        flops=4 * src * 6 * rows * BLOCK * HD,
        transcendentals=src * 6 * rows * BLOCK,
        bytes_accessed=q3.size * 2 + nk * 2 * BLOCK * HD * 2,
    )
    return pl.pallas_call(
        functools.partial(
            attn_kernel, scale=1.0 / math.sqrt(HD), group=group, half=half, parts=len(kv_parts)
        ),
        out_shape=jax.ShapeDtypeStruct((src, BLOCK, width_q), q3.dtype),
        grid_spec=pltpu.PrefetchScalarGridSpec(
            num_scalar_prefetch=3,
            grid=(src,),
            in_specs=[q_spec] + [any_spec] * len(kv_parts),
            out_specs=o_spec,
            scratch_shapes=[
                pltpu.VMEM((nk, 2, BLOCK, HD), jnp.bfloat16),
                pltpu.SemaphoreType.DMA((len(kv_parts),)),
                pltpu.VMEM((width, rows, BLOCK), jnp.float32),
                pltpu.VMEM((rows, BLOCK), jnp.float32),
                pltpu.VMEM((rows, BLOCK), jnp.float32),
                pltpu.VMEM((rows, HD), jnp.float32),
            ],
        ),
        compiler_params=pltpu.CompilerParams(
            dimension_semantics=("arbitrary",), vmem_limit_bytes=48 * 1024 * 1024
        ),
        cost_estimate=cost,
    )(kidx, cnt, order, q3, *kv_parts)


def _copy_kernel(x_ref, o_ref):
    o_ref[...] = x_ref[...].reshape(o_ref.shape)


def _rot_copy_kernel(rot_ref, x_ref, o_ref):
    o_ref[...] = x_ref[...].reshape(o_ref.shape)


def split_columns(x, parts, rot):
    rows, cols = x.shape
    width = cols // parts
    return pl.pallas_call(
        _rot_copy_kernel,
        out_shape=jax.ShapeDtypeStruct((parts, rows, width), x.dtype),
        grid_spec=pltpu.PrefetchScalarGridSpec(
            num_scalar_prefetch=1,
            grid=(parts,),
            in_specs=[pl.BlockSpec((rows, width), lambda k, rot: (0, (k + rot[0]) % parts))],
            out_specs=pl.BlockSpec((1, rows, width), lambda k, rot: (k, 0, 0)),
        ),
        cost_estimate=pl.CostEstimate(flops=0, transcendentals=0, bytes_accessed=2 * x.size * 2),
    )(rot, x)


def _join_kernel(*refs):
    o_ref = refs[-1]
    rows = refs[0].shape[1]
    for h, x_ref in enumerate(refs[:-1]):
        o_ref[h * rows:(h + 1) * rows, :] = x_ref[0]


def join_columns(parts):
    count, rows, width = parts[0].shape
    total = rows * len(parts)
    return pl.pallas_call(
        _join_kernel,
        out_shape=jax.ShapeDtypeStruct((total, count * width), parts[0].dtype),
        grid=(count,),
        in_specs=[pl.BlockSpec((1, rows, width), lambda k: (k, 0, 0))] * len(parts),
        out_specs=pl.BlockSpec((total, width), lambda k: (0, k)),
        cost_estimate=pl.CostEstimate(
            flops=0, transcendentals=0, bytes_accessed=4 * parts[0].size * len(parts)
        ),
    )(*parts)


def shards(queries, key_states, value_states, page_ids, ref_group, ref_slot):
    n_head = lax.axis_size("head")
    n_ctx = lax.axis_size("ctx")
    tokens = queries.shape[0]
    kv_width = key_states.shape[1]
    kv_heads = kv_width // HD
    q_width = queries.shape[1] // kv_heads
    halves = tokens // BLOCK
    blocks = n_head * halves
    refs = ref_group.shape[1]
    cap = blocks * refs // n_ctx

    kv4 = jnp.stack(
        [
            key_states.reshape(tokens, kv_heads, HD).transpose(1, 0, 2),
            value_states.reshape(tokens, kv_heads, HD).transpose(1, 0, 2),
        ],
        axis=1,
    )
    kv_here = lax.all_to_all(kv4, "head", split_axis=0, concat_axis=0, tiled=True)
    me_h = lax.axis_index("head")
    rot = jnp.reshape(me_h, (1,)).astype(jnp.int32)
    kv_here, q_rot = lax.optimization_barrier((kv_here, split_columns(queries, kv_heads, rot)))
    own_kv = (
        kv_here.reshape(n_head, 2, halves, BLOCK, HD).transpose(0, 2, 1, 3, 4).reshape(blocks, 2, BLOCK, HD)
    )

    me = lax.axis_index("ctx")
    rg = ref_group.reshape(n_ctx, blocks * refs)
    rs = ref_slot.reshape(n_ctx, blocks * refs)
    hit = (rg[:, :, None] == jnp.arange(n_ctx, dtype=jnp.int32)[None, None, :]).astype(jnp.int32)
    rank = jnp.sum((jnp.cumsum(hit, axis=1) - 1) * hit, axis=2)
    pick = (rg == me)[:, :, None] & (rank[:, :, None] == jnp.arange(cap, dtype=jnp.int32)[None, None, :])
    send_idx = jnp.sum(jnp.where(pick, rs[:, :, None], 0), axis=1)
    send_kv = jnp.take(own_kv, send_idx.reshape(-1), axis=0, mode="clip").reshape(n_ctx, cap, 2, BLOCK, HD)
    recv_kv = lax.all_to_all(send_kv, "ctx", split_axis=0, concat_axis=0, tiled=True)

    q_t, _ = lax.optimization_barrier((q_rot, send_kv))
    q_shift = [q_t[0]]
    for k in range(1, n_head):
        q_shift.append(lax.ppermute(q_t[k], "head", [(h, (h + k) % n_head) for h in range(n_head)]))
    q_here = jnp.stack(q_shift, axis=0)
    order = ((me_h - jnp.arange(n_head, dtype=jnp.int32)) % n_head).astype(jnp.int32)

    route = [(g, g + 1) for g in range(n_ctx - 1)]
    tail_kv = lax.ppermute(own_kv[blocks - TAIL:], "ctx", route)
    kv_parts = [tail_kv, own_kv, recv_kv.reshape(n_ctx * cap, 2, BLOCK, HD)]

    starts = page_starts(page_ids)
    first = me * blocks
    local = jnp.arange(blocks, dtype=jnp.int32)
    gblock = first + local
    st = lax.dynamic_slice_in_dim(starts, first, blocks, 0)
    near_t = jnp.arange(MAXPAGE, dtype=jnp.int32)
    near_ok = (near_t[None, :] == 0) | (near_t[None, :] <= (gblock - st)[:, None])
    near_idx = jnp.where(near_t[None, :] == 0, (local + TAIL)[:, None], (st - first + TAIL - 1)[:, None] + near_t[None, :])
    my_rg = lax.dynamic_slice_in_dim(ref_group, first, blocks, 0)
    my_rs = lax.dynamic_slice_in_dim(ref_slot, first, blocks, 0)
    my_rank = lax.dynamic_index_in_dim(rank, me, 0, keepdims=False).reshape(blocks, refs)
    ref_ok = (my_rg * blocks + my_rs) < st[:, None]
    ref_idx = TAIL + blocks + my_rg * cap + my_rank
    cand = jnp.concatenate([near_idx, ref_idx], axis=1)
    ok = jnp.concatenate([near_ok, ref_ok], axis=1)
    pos = jnp.cumsum(ok.astype(jnp.int32), axis=1) - 1
    width = MAXPAGE + refs
    slot = jnp.arange(width, dtype=jnp.int32)
    place = ok[:, :, None] & (pos[:, :, None] == slot[None, None, :])
    kidx = jnp.sum(jnp.where(place, cand[:, :, None], 0), axis=1).astype(jnp.int32)
    cnt = jnp.sum(ok.astype(jnp.int32), axis=1).astype(jnp.int32)

    outs = []
    for h in range(halves):
        out_h = attention(kidx, cnt, order, q_here, kv_parts, h)
        outs.append(lax.all_to_all(out_h, "head", split_axis=0, concat_axis=0, tiled=True))
    return join_columns(outs)


def solution(mesh):
    placed = (
        P(("ctx", "head"), None),
        P(("ctx", "head"), None),
        P(("ctx", "head"), None),
        P(),
        P(),
        P(),
    )
    return jax.shard_map(
        shards, mesh=mesh, in_specs=placed, out_specs=P(("ctx", "head"), None), check_vma=False
    )
```

```python
import functools
import math

import jax
import jax.numpy as jnp
from jax import lax
from jax.experimental import pallas as pl
from jax.experimental.pallas import tpu as pltpu
from jax.sharding import PartitionSpec as P

HD = 128
BLOCK = 128
MAXPAGE = 8
TAIL = MAXPAGE - 1


def page_starts(page_ids):
    block_count = page_ids.shape[0]
    position = jnp.arange(block_count, dtype=jnp.int32)
    is_fresh = jnp.concatenate([jnp.ones((1,), dtype=jnp.bool_), page_ids[1:] != page_ids[:-1]])
    return lax.cummax(jnp.where(is_fresh, position, jnp.zeros_like(position)), axis=0)


def attn_kernel(kidx_ref, cnt_ref, order_ref, q_ref, *rest, scale, group, half, parts):
    kv_parts = rest[:parts]
    o_ref = rest[parts]
    kv_ref, sem, s_scr, m_scr, l_scr, acc_scr = rest[parts + 1:]
    j = pl.program_id(0)

    @pl.when(j == 0)
    def _():
        copies = []
        start = 0
        for idx, part in enumerate(kv_parts):
            size = part.shape[0]
            copy = pltpu.make_async_copy(part, kv_ref.at[pl.ds(start, size)], sem.at[idx])
            copy.start()
            copies.append(copy)
            start += size
        for copy in copies:
            copy.wait()

    b = order_ref[j] * 2 + half
    n = cnt_ref[b]
    diag = TAIL + b
    rows = group * BLOCK
    q_tile = q_ref[0]
    q = jnp.concatenate([q_tile[:, h * HD:(h + 1) * HD] for h in range(group)], axis=0)
    tok = lax.broadcasted_iota(jnp.int32, (rows, BLOCK), 0) % BLOCK
    ahead = lax.broadcasted_iota(jnp.int32, (rows, BLOCK), 1) - tok
    dims = (((1,), (1,)), ((), ()))

    def pair(t, which):
        return jnp.concatenate(
            [kv_ref[kidx_ref[b, t], which], kv_ref[kidx_ref[b, t + 1], which]], axis=0
        )

    s = lax.dot_general(q, kv_ref[diag, 0], dims, preferred_element_type=jnp.float32) * scale
    s = jnp.where(ahead <= 0, s, -1e30)
    s_scr[0] = s
    m_scr[...] = s
    rest = n - 1
    pairs = rest // 2

    def scores(p, carry):
        t = 1 + 2 * p
        s = lax.dot_general(q, pair(t, 0), dims, preferred_element_type=jnp.float32) * scale
        s_scr[t] = s[:, :BLOCK]
        s_scr[t + 1] = s[:, BLOCK:]
        m_scr[...] = jnp.maximum(m_scr[...], jnp.maximum(s[:, :BLOCK], s[:, BLOCK:]))
        return carry

    lax.fori_loop(0, pairs, scores, 0)

    @pl.when(rest % 2 == 1)
    def _():
        t = n - 1
        s = lax.dot_general(q, kv_ref[kidx_ref[b, t], 0], dims, preferred_element_type=jnp.float32) * scale
        s_scr[t] = s
        m_scr[...] = jnp.maximum(m_scr[...], s)

    m = jnp.max(m_scr[...], axis=1, keepdims=True)

    p0 = jnp.exp(s_scr[0] - m)
    l_scr[...] = p0
    acc_scr[...] = jnp.dot(p0.astype(jnp.bfloat16), kv_ref[diag, 1], preferred_element_type=jnp.float32)

    def mix(p, carry):
        t = 1 + 2 * p
        p1 = jnp.exp(s_scr[t] - m)
        p2 = jnp.exp(s_scr[t + 1] - m)
        l_scr[...] += p1 + p2
        w = jnp.concatenate([p1, p2], axis=1).astype(jnp.bfloat16)
        acc_scr[...] += jnp.dot(w, pair(t, 1), preferred_element_type=jnp.float32)
        return carry

    lax.fori_loop(0, pairs, mix, 0)

    @pl.when(rest % 2 == 1)
    def _():
        t = n - 1
        p1 = jnp.exp(s_scr[t] - m)
        l_scr[...] += p1
        acc_scr[...] += jnp.dot(
            p1.astype(jnp.bfloat16), kv_ref[kidx_ref[b, t], 1], preferred_element_type=jnp.float32
        )

    total = jnp.sum(l_scr[...], axis=1, keepdims=True)
    out = acc_scr[...] / total
    for h in range(group):
        o_ref[0, :, h * HD:(h + 1) * HD] = out[h * BLOCK:(h + 1) * BLOCK].astype(o_ref.dtype)


def attention(kidx, cnt, order, q3, kv_parts, half):
    src, width_q = q3.shape[0], q3.shape[2]
    group = width_q // HD
    nk = sum(part.shape[0] for part in kv_parts)
    width = kidx.shape[1]
    rows = group * BLOCK
    q_spec = pl.BlockSpec((1, BLOCK, width_q), lambda j, kidx, cnt, order: (j, half, 0))
    o_spec = pl.BlockSpec((1, BLOCK, width_q), lambda j, kidx, cnt, order: (order[j], 0, 0))
    any_spec = pl.BlockSpec(memory_space=pl.ANY)
    cost = pl.CostEstimate(
        flops=4 * src * 6 * rows * BLOCK * HD,
        transcendentals=src * 6 * rows * BLOCK,
        bytes_accessed=q3.size * 2 + nk * 2 * BLOCK * HD * 2,
    )
    return pl.pallas_call(
        functools.partial(
            attn_kernel, scale=1.0 / math.sqrt(HD), group=group, half=half, parts=len(kv_parts)
        ),
        out_shape=jax.ShapeDtypeStruct((src, BLOCK, width_q), q3.dtype),
        grid_spec=pltpu.PrefetchScalarGridSpec(
            num_scalar_prefetch=3,
            grid=(src,),
            in_specs=[q_spec] + [any_spec] * len(kv_parts),
            out_specs=o_spec,
            scratch_shapes=[
                pltpu.VMEM((nk, 2, BLOCK, HD), jnp.bfloat16),
                pltpu.SemaphoreType.DMA((len(kv_parts),)),
                pltpu.VMEM((width, rows, BLOCK), jnp.float32),
                pltpu.VMEM((rows, BLOCK), jnp.float32),
                pltpu.VMEM((rows, BLOCK), jnp.float32),
                pltpu.VMEM((rows, HD), jnp.float32),
            ],
        ),
        compiler_params=pltpu.CompilerParams(
            dimension_semantics=("arbitrary",), vmem_limit_bytes=48 * 1024 * 1024
        ),
        cost_estimate=cost,
    )(kidx, cnt, order, q3, *kv_parts)


def _copy_kernel(x_ref, o_ref):
    o_ref[...] = x_ref[...].reshape(o_ref.shape)


def split_columns(x, parts):
    rows, cols = x.shape
    width = cols // parts
    return pl.pallas_call(
        _copy_kernel,
        out_shape=jax.ShapeDtypeStruct((parts, rows, width), x.dtype),
        grid=(parts,),
        in_specs=[pl.BlockSpec((rows, width), lambda k: (0, k))],
        out_specs=pl.BlockSpec((1, rows, width), lambda k: (k, 0, 0)),
        cost_estimate=pl.CostEstimate(flops=0, transcendentals=0, bytes_accessed=2 * x.size * 2),
    )(x)


def _join_kernel(*refs):
    o_ref = refs[-1]
    per, rows, width = refs[0].shape
    for h, x_ref in enumerate(refs[:-1]):
        for c in range(per):
            o_ref[h * rows:(h + 1) * rows, c * width:(c + 1) * width] = x_ref[c]


def join_columns(parts, per=4):
    count, rows, width = parts[0].shape
    total = rows * len(parts)
    return pl.pallas_call(
        _join_kernel,
        out_shape=jax.ShapeDtypeStruct((total, count * width), parts[0].dtype),
        grid=(count // per,),
        in_specs=[pl.BlockSpec((per, rows, width), lambda k: (k, 0, 0))] * len(parts),
        out_specs=pl.BlockSpec((total, per * width), lambda k: (0, k)),
        cost_estimate=pl.CostEstimate(
            flops=0, transcendentals=0, bytes_accessed=4 * parts[0].size * len(parts)
        ),
    )(*parts)


def shards(queries, key_states, value_states, page_ids, ref_group, ref_slot):
    n_head = lax.axis_size("head")
    n_ctx = lax.axis_size("ctx")
    tokens = queries.shape[0]
    kv_width = key_states.shape[1]
    kv_heads = kv_width // HD
    q_width = queries.shape[1] // kv_heads
    halves = tokens // BLOCK
    blocks = n_head * halves
    refs = ref_group.shape[1]
    cap = blocks * refs // n_ctx

    kv4 = jnp.stack(
        [
            key_states.reshape(tokens, kv_heads, HD).transpose(1, 0, 2),
            value_states.reshape(tokens, kv_heads, HD).transpose(1, 0, 2),
        ],
        axis=1,
    )
    kv_here = lax.all_to_all(kv4, "head", split_axis=0, concat_axis=0, tiled=True)
    own_kv = (
        kv_here.reshape(n_head, 2, halves, BLOCK, HD).transpose(0, 2, 1, 3, 4).reshape(blocks, 2, BLOCK, HD)
    )

    me = lax.axis_index("ctx")
    rg = ref_group.reshape(n_ctx, blocks * refs)
    rs = ref_slot.reshape(n_ctx, blocks * refs)
    hit = (rg[:, :, None] == jnp.arange(n_ctx, dtype=jnp.int32)[None, None, :]).astype(jnp.int32)
    rank = jnp.sum((jnp.cumsum(hit, axis=1) - 1) * hit, axis=2)
    pick = (rg == me)[:, :, None] & (rank[:, :, None] == jnp.arange(cap, dtype=jnp.int32)[None, None, :])
    send_idx = jnp.sum(jnp.where(pick, rs[:, :, None], 0), axis=1)
    send_kv = jnp.take(own_kv, send_idx.reshape(-1), axis=0, mode="clip").reshape(n_ctx, cap, 2, BLOCK, HD)
    recv_kv = lax.all_to_all(send_kv, "ctx", split_axis=0, concat_axis=0, tiled=True)

    q_t, _ = lax.optimization_barrier((split_columns(queries, kv_heads), send_kv))
    me_h = lax.axis_index("head")
    q_shift = [lax.dynamic_index_in_dim(q_t, me_h, 0, keepdims=False)]
    for k in range(1, n_head):
        piece = lax.dynamic_index_in_dim(q_t, (me_h + k) % n_head, 0, keepdims=False)
        q_shift.append(lax.ppermute(piece, "head", [(h, (h + k) % n_head) for h in range(n_head)]))
    q_here = jnp.stack(q_shift, axis=0)
    order = ((me_h - jnp.arange(n_head, dtype=jnp.int32)) % n_head).astype(jnp.int32)

    route = [(g, g + 1) for g in range(n_ctx - 1)]
    tail_kv = lax.ppermute(own_kv[blocks - TAIL:], "ctx", route)
    kv_parts = [tail_kv, own_kv, recv_kv.reshape(n_ctx * cap, 2, BLOCK, HD)]

    starts = page_starts(page_ids)
    first = me * blocks
    local = jnp.arange(blocks, dtype=jnp.int32)
    gblock = first + local
    st = lax.dynamic_slice_in_dim(starts, first, blocks, 0)
    near_t = jnp.arange(MAXPAGE, dtype=jnp.int32)
    near_ok = (near_t[None, :] == 0) | (near_t[None, :] <= (gblock - st)[:, None])
    near_idx = jnp.where(near_t[None, :] == 0, (local + TAIL)[:, None], (st - first + TAIL - 1)[:, None] + near_t[None, :])
    my_rg = lax.dynamic_slice_in_dim(ref_group, first, blocks, 0)
    my_rs = lax.dynamic_slice_in_dim(ref_slot, first, blocks, 0)
    my_rank = lax.dynamic_index_in_dim(rank, me, 0, keepdims=False).reshape(blocks, refs)
    ref_ok = (my_rg * blocks + my_rs) < st[:, None]
    ref_idx = TAIL + blocks + my_rg * cap + my_rank
    cand = jnp.concatenate([near_idx, ref_idx], axis=1)
    ok = jnp.concatenate([near_ok, ref_ok], axis=1)
    pos = jnp.cumsum(ok.astype(jnp.int32), axis=1) - 1
    width = MAXPAGE + refs
    slot = jnp.arange(width, dtype=jnp.int32)
    place = ok[:, :, None] & (pos[:, :, None] == slot[None, None, :])
    kidx = jnp.sum(jnp.where(place, cand[:, :, None], 0), axis=1).astype(jnp.int32)
    cnt = jnp.sum(ok.astype(jnp.int32), axis=1).astype(jnp.int32)

    outs = []
    for h in range(halves):
        out_h = attention(kidx, cnt, order, q_here, kv_parts, h)
        outs.append(lax.all_to_all(out_h, "head", split_axis=0, concat_axis=0, tiled=True))
    return join_columns(outs)


def solution(mesh):
    placed = (
        P(("ctx", "head"), None),
        P(("ctx", "head"), None),
        P(("ctx", "head"), None),
        P(),
        P(),
        P(),
    )
    return jax.shard_map(
        shards, mesh=mesh, in_specs=placed, out_specs=P(("ctx", "head"), None), check_vma=False
    )
```

```python
import functools
import math

import jax
import jax.numpy as jnp
from jax import lax
from jax.experimental import pallas as pl
from jax.experimental.pallas import tpu as pltpu
from jax.sharding import PartitionSpec as P

HD = 128
BLOCK = 128
MAXPAGE = 8
TAIL = MAXPAGE - 1


def page_starts(page_ids):
    block_count = page_ids.shape[0]
    position = jnp.arange(block_count, dtype=jnp.int32)
    is_fresh = jnp.concatenate([jnp.ones((1,), dtype=jnp.bool_), page_ids[1:] != page_ids[:-1]])
    return lax.cummax(jnp.where(is_fresh, position, jnp.zeros_like(position)), axis=0)


def attn_kernel(kidx_ref, cnt_ref, order_ref, q_ref, *rest, scale, group, half, parts):
    kv_parts = rest[:parts]
    o_ref = rest[parts]
    kv_ref, sem, s_scr, m_scr, l_scr, acc_scr = rest[parts + 1:]
    j = pl.program_id(0)

    @pl.when(j == 0)
    def _():
        copies = []
        start = 0
        for idx, part in enumerate(kv_parts):
            size = part.shape[0]
            copy = pltpu.make_async_copy(part, kv_ref.at[pl.ds(start, size)], sem.at[idx])
            copy.start()
            copies.append(copy)
            start += size
        for copy in copies:
            copy.wait()

    b = order_ref[j] * 2 + half
    n = cnt_ref[b]
    diag = TAIL + b
    rows = group * BLOCK
    q_tile = q_ref[0]
    q = jnp.concatenate([q_tile[:, h * HD:(h + 1) * HD] for h in range(group)], axis=0)
    tok = lax.broadcasted_iota(jnp.int32, (rows, BLOCK), 0) % BLOCK
    ahead = lax.broadcasted_iota(jnp.int32, (rows, BLOCK), 1) - tok
    dims = (((1,), (1,)), ((), ()))

    def pair(t, which):
        return jnp.concatenate(
            [kv_ref[kidx_ref[b, t], which], kv_ref[kidx_ref[b, t + 1], which]], axis=0
        )

    s = lax.dot_general(q, kv_ref[diag, 0], dims, preferred_element_type=jnp.float32) * scale
    s = jnp.where(ahead <= 0, s, -1e30)
    s_scr[0] = s
    m_scr[...] = s
    rest = n - 1
    pairs = rest // 2

    def scores(p, carry):
        t = 1 + 2 * p
        s = lax.dot_general(q, pair(t, 0), dims, preferred_element_type=jnp.float32) * scale
        s_scr[t] = s[:, :BLOCK]
        s_scr[t + 1] = s[:, BLOCK:]
        m_scr[...] = jnp.maximum(m_scr[...], jnp.maximum(s[:, :BLOCK], s[:, BLOCK:]))
        return carry

    lax.fori_loop(0, pairs, scores, 0)

    @pl.when(rest % 2 == 1)
    def _():
        t = n - 1
        s = lax.dot_general(q, kv_ref[kidx_ref[b, t], 0], dims, preferred_element_type=jnp.float32) * scale
        s_scr[t] = s
        m_scr[...] = jnp.maximum(m_scr[...], s)

    m = jnp.max(m_scr[...], axis=1, keepdims=True)

    p0 = jnp.exp(s_scr[0] - m)
    l_scr[...] = p0
    acc_scr[...] = jnp.dot(p0.astype(jnp.bfloat16), kv_ref[diag, 1], preferred_element_type=jnp.float32)

    def mix(p, carry):
        t = 1 + 2 * p
        p1 = jnp.exp(s_scr[t] - m)
        p2 = jnp.exp(s_scr[t + 1] - m)
        l_scr[...] += p1 + p2
        w = jnp.concatenate([p1, p2], axis=1).astype(jnp.bfloat16)
        acc_scr[...] += jnp.dot(w, pair(t, 1), preferred_element_type=jnp.float32)
        return carry

    lax.fori_loop(0, pairs, mix, 0)

    @pl.when(rest % 2 == 1)
    def _():
        t = n - 1
        p1 = jnp.exp(s_scr[t] - m)
        l_scr[...] += p1
        acc_scr[...] += jnp.dot(
            p1.astype(jnp.bfloat16), kv_ref[kidx_ref[b, t], 1], preferred_element_type=jnp.float32
        )

    total = jnp.sum(l_scr[...], axis=1, keepdims=True)
    out = acc_scr[...] / total
    for h in range(group):
        o_ref[0, :, h * HD:(h + 1) * HD] = out[h * BLOCK:(h + 1) * BLOCK].astype(o_ref.dtype)


def attention(kidx, cnt, order, q3, kv_parts, half):
    src, width_q = q3.shape[0], q3.shape[2]
    group = width_q // HD
    nk = sum(part.shape[0] for part in kv_parts)
    width = kidx.shape[1]
    rows = group * BLOCK
    q_spec = pl.BlockSpec((1, BLOCK, width_q), lambda j, kidx, cnt, order: (j, half, 0))
    o_spec = pl.BlockSpec((1, BLOCK, width_q), lambda j, kidx, cnt, order: (order[j], 0, 0))
    any_spec = pl.BlockSpec(memory_space=pl.ANY)
    cost = pl.CostEstimate(
        flops=4 * src * 6 * rows * BLOCK * HD,
        transcendentals=src * 6 * rows * BLOCK,
        bytes_accessed=q3.size * 2 + nk * 2 * BLOCK * HD * 2,
    )
    return pl.pallas_call(
        functools.partial(
            attn_kernel, scale=1.0 / math.sqrt(HD), group=group, half=half, parts=len(kv_parts)
        ),
        out_shape=jax.ShapeDtypeStruct((src, BLOCK, width_q), q3.dtype),
        grid_spec=pltpu.PrefetchScalarGridSpec(
            num_scalar_prefetch=3,
            grid=(src,),
            in_specs=[q_spec] + [any_spec] * len(kv_parts),
            out_specs=o_spec,
            scratch_shapes=[
                pltpu.VMEM((nk, 2, BLOCK, HD), jnp.bfloat16),
                pltpu.SemaphoreType.DMA((len(kv_parts),)),
                pltpu.VMEM((width, rows, BLOCK), jnp.float32),
                pltpu.VMEM((rows, BLOCK), jnp.float32),
                pltpu.VMEM((rows, BLOCK), jnp.float32),
                pltpu.VMEM((rows, HD), jnp.float32),
            ],
        ),
        compiler_params=pltpu.CompilerParams(
            dimension_semantics=("arbitrary",), vmem_limit_bytes=48 * 1024 * 1024
        ),
        cost_estimate=cost,
    )(kidx, cnt, order, q3, *kv_parts)


def _copy_kernel(x_ref, o_ref):
    width = o_ref.shape[2]
    for c in range(o_ref.shape[0]):
        o_ref[c] = x_ref[:, c * width:(c + 1) * width]


def split_columns(x, parts, per=4):
    rows, cols = x.shape
    width = cols // parts
    return pl.pallas_call(
        _copy_kernel,
        out_shape=jax.ShapeDtypeStruct((parts, rows, width), x.dtype),
        grid=(parts // per,),
        in_specs=[pl.BlockSpec((rows, per * width), lambda k: (0, k))],
        out_specs=pl.BlockSpec((per, rows, width), lambda k: (k, 0, 0)),
        cost_estimate=pl.CostEstimate(flops=0, transcendentals=0, bytes_accessed=2 * x.size * 2),
    )(x)


def _join_kernel(*refs):
    o_ref = refs[-1]
    per, rows, width = refs[0].shape
    for h, x_ref in enumerate(refs[:-1]):
        for c in range(per):
            o_ref[h * rows:(h + 1) * rows, c * width:(c + 1) * width] = x_ref[c]


def join_columns(parts, per=4):
    count, rows, width = parts[0].shape
    total = rows * len(parts)
    return pl.pallas_call(
        _join_kernel,
        out_shape=jax.ShapeDtypeStruct((total, count * width), parts[0].dtype),
        grid=(count // per,),
        in_specs=[pl.BlockSpec((per, rows, width), lambda k: (k, 0, 0))] * len(parts),
        out_specs=pl.BlockSpec((total, per * width), lambda k: (0, k)),
        cost_estimate=pl.CostEstimate(
            flops=0, transcendentals=0, bytes_accessed=4 * parts[0].size * len(parts)
        ),
    )(*parts)


def shards(queries, key_states, value_states, page_ids, ref_group, ref_slot):
    n_head = lax.axis_size("head")
    n_ctx = lax.axis_size("ctx")
    tokens = queries.shape[0]
    kv_width = key_states.shape[1]
    kv_heads = kv_width // HD
    q_width = queries.shape[1] // kv_heads
    halves = tokens // BLOCK
    blocks = n_head * halves
    refs = ref_group.shape[1]
    cap = blocks * refs // n_ctx

    kv4 = jnp.stack(
        [
            key_states.reshape(tokens, kv_heads, HD).transpose(1, 0, 2),
            value_states.reshape(tokens, kv_heads, HD).transpose(1, 0, 2),
        ],
        axis=1,
    )
    kv_here = lax.all_to_all(kv4, "head", split_axis=0, concat_axis=0, tiled=True)
    own_kv = (
        kv_here.reshape(n_head, 2, halves, BLOCK, HD).transpose(0, 2, 1, 3, 4).reshape(blocks, 2, BLOCK, HD)
    )

    me = lax.axis_index("ctx")
    rg = ref_group.reshape(n_ctx, blocks * refs)
    rs = ref_slot.reshape(n_ctx, blocks * refs)
    hit = (rg[:, :, None] == jnp.arange(n_ctx, dtype=jnp.int32)[None, None, :]).astype(jnp.int32)
    rank = jnp.sum((jnp.cumsum(hit, axis=1) - 1) * hit, axis=2)
    pick = (rg == me)[:, :, None] & (rank[:, :, None] == jnp.arange(cap, dtype=jnp.int32)[None, None, :])
    send_idx = jnp.sum(jnp.where(pick, rs[:, :, None], 0), axis=1)
    send_kv = jnp.take(own_kv, send_idx.reshape(-1), axis=0, mode="clip").reshape(n_ctx, cap, 2, BLOCK, HD)
    recv_kv = lax.all_to_all(send_kv, "ctx", split_axis=0, concat_axis=0, tiled=True)

    q_t, _ = lax.optimization_barrier((split_columns(queries, kv_heads), send_kv))
    me_h = lax.axis_index("head")
    q_shift = [lax.dynamic_index_in_dim(q_t, me_h, 0, keepdims=False)]
    for k in range(1, n_head):
        piece = lax.dynamic_index_in_dim(q_t, (me_h + k) % n_head, 0, keepdims=False)
        q_shift.append(lax.ppermute(piece, "head", [(h, (h + k) % n_head) for h in range(n_head)]))
    q_here = jnp.stack(q_shift, axis=0)
    order = ((me_h - jnp.arange(n_head, dtype=jnp.int32)) % n_head).astype(jnp.int32)

    route = [(g, g + 1) for g in range(n_ctx - 1)]
    tail_kv = lax.ppermute(own_kv[blocks - TAIL:], "ctx", route)
    kv_parts = [tail_kv, own_kv, recv_kv.reshape(n_ctx * cap, 2, BLOCK, HD)]

    starts = page_starts(page_ids)
    first = me * blocks
    local = jnp.arange(blocks, dtype=jnp.int32)
    gblock = first + local
    st = lax.dynamic_slice_in_dim(starts, first, blocks, 0)
    near_t = jnp.arange(MAXPAGE, dtype=jnp.int32)
    near_ok = (near_t[None, :] == 0) | (near_t[None, :] <= (gblock - st)[:, None])
    near_idx = jnp.where(near_t[None, :] == 0, (local + TAIL)[:, None], (st - first + TAIL - 1)[:, None] + near_t[None, :])
    my_rg = lax.dynamic_slice_in_dim(ref_group, first, blocks, 0)
    my_rs = lax.dynamic_slice_in_dim(ref_slot, first, blocks, 0)
    my_rank = lax.dynamic_index_in_dim(rank, me, 0, keepdims=False).reshape(blocks, refs)
    ref_ok = (my_rg * blocks + my_rs) < st[:, None]
    ref_idx = TAIL + blocks + my_rg * cap + my_rank
    cand = jnp.concatenate([near_idx, ref_idx], axis=1)
    ok = jnp.concatenate([near_ok, ref_ok], axis=1)
    pos = jnp.cumsum(ok.astype(jnp.int32), axis=1) - 1
    width = MAXPAGE + refs
    slot = jnp.arange(width, dtype=jnp.int32)
    place = ok[:, :, None] & (pos[:, :, None] == slot[None, None, :])
    kidx = jnp.sum(jnp.where(place, cand[:, :, None], 0), axis=1).astype(jnp.int32)
    cnt = jnp.sum(ok.astype(jnp.int32), axis=1).astype(jnp.int32)

    outs = []
    for h in range(halves):
        out_h = attention(kidx, cnt, order, q_here, kv_parts, h)
        outs.append(lax.all_to_all(out_h, "head", split_axis=0, concat_axis=0, tiled=True))
    return join_columns(outs)


def solution(mesh):
    placed = (
        P(("ctx", "head"), None),
        P(("ctx", "head"), None),
        P(("ctx", "head"), None),
        P(),
        P(),
        P(),
    )
    return jax.shard_map(
        shards, mesh=mesh, in_specs=placed, out_specs=P(("ctx", "head"), None), check_vma=False
    )
```
